256 devices in a mesh: sect: 2 (over y_lo), batch: 16 (over z, core), head: 8 (over x, y_hi).
Axes of the slice: x: 4, y: 4 (y_hi: 2, y_lo: 2; y = y_hi * 2 + y_lo), z: 8, core: 2. Of those that a mesh axis runs over, the one named last changes fastest.
Arguments:
- queries: bfloat16 [96, 16, 512], P('batch', 'head', 'sect'), may hold values from -51 to 51
- newest_key_value: bfloat16 [96, 4, 256], P('batch'), may hold values from -5 to 5
- page_cache: bfloat16 [96, 256, 64, 256], P('batch', ('sect', 'head')), may hold values from -4 to 4
- lengths: int32 [96], P('batch'), may hold values from 2048 to 4096, as said below
- page_ids: int32 [96, 4, 32], P('batch'), may hold values from 0 to 63, as said below
- out_weight: bfloat16 [8192, 4096], P(('sect', 'head'), 'batch'), may hold values from -0.0625 to 0.0625
- residual: bfloat16 [96, 4096], P(None, 'batch'), may hold values from -2 to 2
- norm_gain: float32 [4096], P('batch'), may hold values from 0.25 to 1.75
- expert_ids: int32 [96, 8], replicated, may hold values from 0 to 63, all different within a row; in each aligned block of 96 rows (0 to 95, 96 to 191, ...) at most 24 rows name the same one
- route_weight: float32 [96, 8], replicated, may hold values from 0.1 to 1
- gate_up_weight: bfloat16 [32, 4096, 2, 3072], P(('sect', 'batch'), None, None, 'head'), may hold values from -0.09375 to 0.09375
- down_weight: bfloat16 [32, 3072, 4096], P(('sect', 'batch'), 'head'), may hold values from -0.15625 to 0.15625
Outputs:
- layer_out: bfloat16 [96, 4096], P(None, 'batch')
The draws below stay inside these ranges and needn't reach their ends.
Inputs may be any that keep to these rules, and one draw needn't show every extreme that they name: `lengths`: some sequence holds exactly 4096 cached tokens and some exactly 2048. `page_ids`: each row lists 32 different pages in ascending order, all below the number of pages that hold the sequence's cached tokens, and always the last of those pages. `expert_ids`: each row names 8 different experts; over all rows no expert is named by more than 24 rows, a bound that some block reaches.
All inputs are finite; a program needn't handle non-finite values.
Results may differ from the reference program's by a relative error of at most 0.025.
Values may be sent and summed in bfloat16 or wider, within the bound.
No kernel may reach another device: no remote copies, remote signals or barrier semaphores. Data moves between devices by JAX's collectives and lax.ppermute only.
A program may use at most 128 MiB of HBM per device.

```python
import math
import jax
import jax.numpy as jnp
import numpy as np
from jax import lax

D = 4096
QUERY_HEADS = 64
KEY_VALUE_HEADS = 4
HEAD_WIDTH = 128
FFE = 1536
EXPERTS = 64
TOPK = 8
PAGE_TOKENS = 64
PAGES_READ = 32
SEQUENCE_PAGES = 64
SEQUENCE_COUNT = 96
CAP = 24


def draw_plan(key):
    base_key = jax.random.fold_in(key, 7001)
    length_key, page_score_key = jax.random.split(base_key)
    lengths = jax.random.randint(length_key, (SEQUENCE_COUNT,), PAGES_READ * PAGE_TOKENS, SEQUENCE_PAGES * PAGE_TOKENS + 1, dtype=jnp.int32)
    lengths = lengths.at[0].set(SEQUENCE_PAGES * PAGE_TOKENS).at[1].set(PAGES_READ * PAGE_TOKENS)
    valid_pages = (lengths + PAGE_TOKENS - 1) // PAGE_TOKENS
    random_jitter = jax.random.randint(page_score_key, (SEQUENCE_COUNT, KEY_VALUE_HEADS, SEQUENCE_PAGES), 0, 65536, dtype=jnp.int32)
    page_index = jnp.arange(SEQUENCE_PAGES, dtype=jnp.int32)
    ranking = (random_jitter + page_index * 1024) * SEQUENCE_PAGES + page_index
    last_page = valid_pages[:, None, None] - 1
    ranking = jnp.where(page_index == last_page, 2 ** 30, ranking)
    ranking = jnp.where(page_index > last_page, -1, ranking)
    unused, picked = lax.top_k(ranking, PAGES_READ)
    return (lengths.astype(jnp.int32), jnp.sort(picked, axis=-1).astype(jnp.int32))


def cache_base(key):
    cache_key = jax.random.fold_in(key, 7002)
    cache_layout = (SEQUENCE_COUNT, KEY_VALUE_HEADS * SEQUENCE_PAGES, PAGE_TOKENS, 2 * HEAD_WIDTH)
    cache_values = jnp.clip(jax.random.normal(cache_key, cache_layout, jnp.float32), -4.0, 4.0)
    return cache_values


def draw_lengths(key, part):
    return draw_plan(key)[0]


def draw_page_ids(key, part):
    return draw_plan(key)[1]


def draw_page_cache(key, part):
    return cache_base(key).astype(jnp.bfloat16)


def draw_queries(key, part):
    query_key = jax.random.fold_in(key, 7003)
    values = jnp.clip(3.0 * jax.random.normal(query_key, (SEQUENCE_COUNT, QUERY_HEADS, HEAD_WIDTH), jnp.float32), -12.0, 12.0)
    values = values.reshape(SEQUENCE_COUNT, KEY_VALUE_HEADS, QUERY_HEADS // KEY_VALUE_HEADS, HEAD_WIDTH).transpose(0, 2, 1, 3)
    return values.reshape(SEQUENCE_COUNT, QUERY_HEADS // KEY_VALUE_HEADS, KEY_VALUE_HEADS * HEAD_WIDTH).astype(jnp.bfloat16)


def block_scale(stream_key, shape, cuts, smallest, top_value):
    gain, own = 1.0, jax.random.fold_in(stream_key, 6)
    for axis_at, shards_of in cuts:
        draws = jnp.exp(jax.random.uniform(jax.random.fold_in(own, axis_at), (shards_of,), jnp.float32, smallest / len(cuts), top_value / len(cuts)))
        gain = gain * jnp.repeat(draws, shape[axis_at] // shards_of).reshape([-1 if axis == axis_at else 1 for axis in range(len(shape))])
    return gain


def assign_block(rng, own, number, rows, number_of, top, limit, skew):
    sequence = jax.random.permutation(rng, number_of)
    heavy_load, common = shares(number_of, rows * top, limit, skew, True), shares(number_of, rows * top, limit, skew, False)
    places = jnp.arange(number_of)

    def named(sizes, offset_by):
        used = int((sizes > 0).sum())
        fixed = max(1, used // 4)
        passed = fixed + (places - fixed + offset_by * (used - fixed)) % max(1, number_of - fixed)
        return jnp.zeros((number_of,), jnp.int32).at[sequence[jnp.where(places < fixed, places, passed)]].set(jnp.asarray(sizes, jnp.int32))

    sizes = jnp.where(number % 4 == 0, named(heavy_load, number // 4), named(common, number - number // 4 - 1))
    mixed = jax.random.permutation(jax.random.fold_in(own, 3), number_of)
    donor, taker = mixed[0:number_of // 2 * 2:2], mixed[1:number_of // 2 * 2:2]
    margin = jnp.minimum(sizes[donor] - 1, limit - sizes[taker]) // 2
    margin = jnp.where((donor == sequence[0]) | (taker == sequence[0]) | (sizes[taker] == 0), 0, jnp.maximum(margin, 0))
    passed = jax.random.randint(jax.random.fold_in(own, 4), (number_of // 2,), 0, 1 << 20) % (margin + 1)
    sizes = sizes.at[donor].add(-passed).at[taker].add(passed)
    labels = jnp.searchsorted(jnp.cumsum(sizes), jnp.arange(rows * top), side="right").astype(jnp.int32)
    grid = labels.reshape(top, rows).T
    grid = grid[jax.random.permutation(jax.random.fold_in(own, 1), rows)]
    offset_by = jax.random.randint(jax.random.fold_in(own, 2), (rows, 1), 0, top)
    return jnp.take_along_axis(grid, (jnp.arange(top)[None, :] + offset_by) % top, axis=1)


def shares(amount, total, limit, skew, full):
    weights = [(1 << 20) // math.isqrt(rank ** skew) + 1 for rank in range(1, amount + 1)]
    largest = limit if full else min(limit, max(-(-total // amount), total * weights[0] // sum(weights)))
    least = 1 if total - largest >= amount - 1 else 0
    holding, spare = [largest] + [least] * (amount - 1), total - largest - least * (amount - 1)
    while spare > 0:
        candidates = [i for i in range(1, amount) if holding[i] < largest] or [i for i in range(1, amount) if holding[i] < limit]
        mass, remaining = sum([weights[i] for i in candidates]), spare
        for i in candidates:
            extra = min(limit - holding[i], max(1, remaining * weights[i] // mass), spare)
            holding[i] = holding[i] + extra
            spare = spare - extra
    return np.array(holding)


def noise(own_key, extent, deviation, most, cuts=(), kind=jnp.bfloat16):
    result = jax.random.normal(own_key, extent, jnp.float32) * deviation
    if len(cuts) > 0:
        result = block_scale(own_key, extent, cuts, -0.22, 0.18) * result
    return jnp.clip(result, min=-most, max=most).astype(kind)


def setup_inputs(seed: int = 0) -> dict:
    splits = jax.random.split(jax.random.key(seed), 13)
    queries = draw_queries(jax.random.fold_in(splits[12], 71), 0)
    newest_key_value = noise(splits[1], (SEQUENCE_COUNT, KEY_VALUE_HEADS, 2 * HEAD_WIDTH), 1.0, 5.0, ((0, 16),))
    page_cache = draw_page_cache(jax.random.fold_in(splits[12], 71), 0)
    lengths = draw_lengths(jax.random.fold_in(splits[12], 71), 0)
    page_ids = draw_page_ids(jax.random.fold_in(splits[12], 71), 0)
    out_weight = noise(splits[5], (QUERY_HEADS * HEAD_WIDTH, D), (QUERY_HEADS * HEAD_WIDTH) ** -0.5, 0.0625, ((0, 16), (1, 16)))
    residual = noise(splits[6], (SEQUENCE_COUNT, D), 0.3, 2.0, ((1, 16),))
    norm_gain = jnp.clip(1.0 + 0.15 * jax.random.normal(splits[7], (D,), jnp.float32), 0.25, 1.75)
    expert_ids_keys = jax.random.split(jax.random.fold_in(splits[8], 1), SEQUENCE_COUNT // SEQUENCE_COUNT)
    expert_ids_turns = jax.random.permutation(jax.random.fold_in(splits[8], 3), SEQUENCE_COUNT // SEQUENCE_COUNT)
    expert_ids = jax.vmap(lambda own, number: assign_block(jax.random.fold_in(splits[8], 2), own, number, SEQUENCE_COUNT, EXPERTS, TOPK, CAP, 2))(expert_ids_keys, expert_ids_turns).reshape((SEQUENCE_COUNT, TOPK))
    route_weight = jnp.clip(jax.random.uniform(splits[9], (SEQUENCE_COUNT, TOPK), jnp.float32, 0.1, 1.0), 0.1, 1.0)
    gate_up_weight = noise(splits[10], (EXPERTS // 2, D, 2, 2 * FFE), D ** -0.5, 0.09375, ((0, 32), (3, 8)))
    down_weight = noise(splits[11], (EXPERTS // 2, 2 * FFE, D), FFE ** -0.5, 0.15625, ((0, 32), (1, 8)))
    return {"queries": queries, "newest_key_value": newest_key_value, "page_cache": page_cache, "lengths": lengths, "page_ids": page_ids, "out_weight": out_weight, "residual": residual, "norm_gain": norm_gain, "expert_ids": expert_ids, "route_weight": route_weight, "gate_up_weight": gate_up_weight, "down_weight": down_weight}


NEG_FILL = -1e+30
NORM_EPS = 1e-06

def attend_one(entries):
    single_query, newest_entry, cache_entries, sequence_length, chosen = entries
    heads_in_group = QUERY_HEADS // KEY_VALUE_HEADS
    scaling = 1.0 / math.sqrt(HEAD_WIDTH)
    query_groups = single_query.reshape(heads_in_group, KEY_VALUE_HEADS, HEAD_WIDTH).transpose(1, 0, 2).astype(jnp.float32)
    cache_entries = cache_entries.reshape(KEY_VALUE_HEADS, SEQUENCE_PAGES, PAGE_TOKENS, 2 * HEAD_WIDTH)
    block_list = jax.vmap(lambda stored, picked: stored[picked])(cache_entries, chosen)
    token_place = chosen[:, :, None] * PAGE_TOKENS + jnp.arange(PAGE_TOKENS, dtype=jnp.int32)[None, None, :]
    usable_pages = (token_place < sequence_length).reshape(KEY_VALUE_HEADS, PAGES_READ * PAGE_TOKENS)
    usable_pages = jnp.concatenate([usable_pages, jnp.ones((KEY_VALUE_HEADS, 1), dtype=jnp.bool_)], axis=1)
    gathered_keys = jnp.concatenate([block_list[..., :HEAD_WIDTH].reshape(KEY_VALUE_HEADS, PAGES_READ * PAGE_TOKENS, HEAD_WIDTH), newest_entry[:, None, :HEAD_WIDTH]], axis=1).astype(jnp.float32)
    gathered_values = jnp.concatenate([block_list[..., HEAD_WIDTH:].reshape(KEY_VALUE_HEADS, PAGES_READ * PAGE_TOKENS, HEAD_WIDTH), newest_entry[:, None, HEAD_WIDTH:]], axis=1).astype(jnp.float32)
    scores = jnp.einsum('ghd,gkd->ghk', query_groups, gathered_keys) * scaling
    scores = jnp.where(usable_pages[:, None, :], scores, NEG_FILL)
    row_peak = lax.optimization_barrier(jnp.max(scores, axis=2, keepdims=True))
    weights = jnp.where(usable_pages[:, None, :], jnp.exp(scores - row_peak), 0.0)
    totals = lax.optimization_barrier(jnp.sum(weights, axis=2))
    rounded = weights.astype(jnp.bfloat16).astype(jnp.float32)
    mixture = jnp.einsum('ghk,gkd->ghd', rounded, gathered_values) / totals[..., None]
    return mixture.reshape(QUERY_HEADS * HEAD_WIDTH).astype(jnp.bfloat16)

def expert_one(inputs, gate_up, down_part):
    mixture = jnp.dot(inputs, gate_up.reshape(D, 2 * FFE), preferred_element_type=jnp.float32)
    activated = (jax.nn.silu(mixture[:, :FFE]) * mixture[:, FFE:]).astype(jnp.bfloat16)
    return jnp.dot(activated, down_part, preferred_element_type=jnp.float32)

def pair_pass(entries):
    inputs, gate_up, down_part = entries
    first = expert_one(inputs[0], gate_up[:, :, :FFE], down_part[:FFE])
    second = expert_one(inputs[1], gate_up[:, :, FFE:], down_part[FFE:])
    return jnp.stack([first, second])

def reference(queries, newest_key_value, page_cache, lengths, page_ids, out_weight, residual, norm_gain, expert_ids, route_weight, gate_up_weight, down_weight):
    attention = lax.map(attend_one, (queries, newest_key_value, page_cache, lengths, page_ids))
    projected = jnp.dot(attention, out_weight, preferred_element_type=jnp.float32)
    hidden_state = residual.astype(jnp.float32) + projected
    inverse = lax.rsqrt(lax.optimization_barrier(jnp.mean(hidden_state * hidden_state, axis=1)) + NORM_EPS)
    normed = (hidden_state * inverse[:, None] * norm_gain[None, :]).astype(jnp.bfloat16)
    flat_ids = expert_ids.reshape(-1)
    one_hot = (flat_ids[:, None] == jnp.arange(EXPERTS, dtype=jnp.int32)[None, :]).astype(jnp.int32)
    rank_in = lax.optimization_barrier(jnp.sum((jnp.cumsum(one_hot, axis=0) - one_hot) * one_hot, axis=1))
    slot_index = (flat_ids * CAP + rank_in).astype(jnp.int32)
    token_index = jnp.repeat(jnp.arange(SEQUENCE_COUNT, dtype=jnp.int32), TOPK)
    dispatched = jnp.zeros((EXPERTS * CAP, D), jnp.bfloat16).at[slot_index].set(normed[token_index])
    dispatched = dispatched.reshape(EXPERTS // 2, 2, CAP, D)
    outputs = lax.map(pair_pass, (dispatched, gate_up_weight, down_weight)).reshape(EXPERTS * CAP, D)
    gathered = outputs[slot_index].reshape(SEQUENCE_COUNT, TOPK, D)
    coefficient = route_weight / lax.optimization_barrier(jnp.sum(route_weight, axis=1, keepdims=True))
    expert_mix = lax.optimization_barrier(jnp.sum(coefficient[:, :, None] * gathered, axis=1))
    return (hidden_state + expert_mix).astype(jnp.bfloat16)
```

```python
import math

import jax
import jax.numpy as jnp
from jax import lax
from jax.sharding import PartitionSpec as P

D = 4096
EXPERTS = 64


NEG_FILL = -1e30
NORM_EPS = 1e-06


def copy_for_each(shard, axis):
    copies = jnp.broadcast_to(shard, (lax.axis_size(axis), *shard.shape))
    return lax.all_to_all(copies, axis, split_axis=0, concat_axis=0, tiled=True)


def in_order(pieces, dim):
    lengths = list(pieces.shape[1:])
    lengths[dim] *= pieces.shape[0]
    return jnp.moveaxis(pieces, 0, dim).reshape(lengths)


def gathered_copies(shard, axis, dim):
    pieces = copy_for_each(shard, axis)
    return in_order(pieces, dim)


def from_partner(shard, axis, distance):
    return lax.ppermute(shard, axis, [(i, i ^ 1 << distance) for i in range(lax.axis_size(axis))])


def taken_together(shard, axis):
    return copy_for_each(shard, axis).astype(jnp.float32).sum(axis=0)


def of_everyone(shard, axis):
    return copy_for_each(shard, axis).sum(axis=0)


def merge_pair(first, second):
    first_max, first_sum, first_acc = first
    second_max, second_sum, second_acc = second
    joined = jnp.maximum(first_max, second_max)
    first_factor = jnp.exp(first_max - joined)
    second_factor = jnp.exp(second_max - joined)
    return (
        joined,
        first_sum * first_factor + second_sum * second_factor,
        first_acc * first_factor[..., None] + second_acc * second_factor[..., None],
    )


def head_slice(partial_value, begin_at, span_size):
    return tuple(
        (lax.dynamic_slice_in_dim(member, begin_at, span_size, 1) for member in partial_value)
    )


def on_device(
    queries,
    newest_key_value,
    page_cache,
    lengths,
    page_ids,
    out_weight,
    residual,
    norm_gain,
    expert_ids,
    route_weight,
    gate_up_weight,
    down_weight,
):
    seq_count = queries.shape[0]
    head_dim = newest_key_value.shape[2] // 2
    kv_heads = newest_key_value.shape[1]
    sect_size = lax.axis_size("sect")
    head_size = lax.axis_size("head")
    batch_size = lax.axis_size("batch")
    group_size = sect_size * head_size // kv_heads
    position = lax.axis_index("sect") * head_size + lax.axis_index("head")
    kv_index = position // group_size
    quarter = position % group_size
    local_pages = page_cache.shape[1]
    page_len = page_cache.shape[2]
    scaling = 1.0 / math.sqrt(head_dim)
    all_heads = lax.all_gather(queries, "head", axis=1, tiled=True)
    kv_local = kv_index % (kv_heads // sect_size)
    group_query = lax.dynamic_slice_in_dim(all_heads, kv_local * head_dim, head_dim, 2)
    heads_dev = all_heads.shape[1] // group_size
    block_cols = heads_dev * head_dim
    chosen = lax.dynamic_index_in_dim(page_ids, kv_index, 1, keepdims=False)
    leading_page = quarter * local_pages
    page_number = jnp.broadcast_to(
        leading_page + jnp.arange(local_pages, dtype=jnp.int32), (seq_count, local_pages)
    )
    page_used = jnp.any(chosen[:, :, None] == page_number[:, None, :], axis=1)
    token_place = (
        page_number[:, :, None] * page_len + jnp.arange(page_len, dtype=jnp.int32)[None, None, :]
    )
    key_count = page_cache.shape[1] * page_len
    usable_pages = (page_used[:, :, None] & (token_place < lengths[:, None, None])).reshape(
        seq_count, key_count
    )
    gathered_keys = page_cache[..., :head_dim].reshape(seq_count, key_count, head_dim)
    gathered_values = page_cache[..., head_dim:].reshape(seq_count, key_count, head_dim)
    scores = (
        jnp.einsum("shd,skd->shk", group_query, gathered_keys, preferred_element_type=jnp.float32)
        * scaling
    )
    scores = jnp.where(usable_pages[:, None, :], scores, NEG_FILL)
    newest_entry = lax.dynamic_index_in_dim(newest_key_value, kv_index, 1, keepdims=False)
    fresh_score = (
        jnp.einsum(
            "shd,sd->sh",
            group_query,
            newest_entry[:, :head_dim],
            preferred_element_type=jnp.float32,
        )
        * scaling
    )
    leading = quarter == 0
    fresh_score = jnp.where(leading, fresh_score, NEG_FILL)
    running_max = jnp.maximum(jnp.max(scores, axis=2), fresh_score)
    weights = jnp.where(usable_pages[:, None, :], jnp.exp(scores - running_max[..., None]), 0.0)
    fresh_weight = jnp.where(leading, jnp.exp(fresh_score - running_max), 0.0)
    running_sum = jnp.sum(weights, axis=2) + fresh_weight
    weighted = jnp.einsum(
        "shk,skd->shd",
        weights.astype(jnp.bfloat16),
        gathered_values,
        preferred_element_type=jnp.float32,
    )
    weighted = weighted + fresh_weight.astype(jnp.bfloat16).astype(jnp.float32)[
        ..., None
    ] * newest_entry[:, None, head_dim:].astype(jnp.float32)
    partial_value = (running_max, running_sum, weighted)
    bit_count = group_size.bit_length() - 1
    for bit_index in reversed(range(bit_count)):
        half_heads = partial_value[0].shape[1] // 2
        keep_half = quarter >> bit_index & 1
        kept = head_slice(partial_value, keep_half * half_heads, half_heads)
        sent = head_slice(partial_value, (1 - keep_half) * half_heads, half_heads)
        partner = from_partner(sent, "head", bit_index)
        partial_value = merge_pair(kept, partner)
    attention = (
        (partial_value[2] / partial_value[1][..., None])
        .reshape(seq_count, block_cols)
        .astype(jnp.bfloat16)
    )
    head_terms = jnp.dot(
        lax.all_gather(attention, "batch", axis=0, tiled=True),
        out_weight,
        preferred_element_type=jnp.float32,
    )
    projected = lax.psum(head_terms, ("sect", "head"))
    hidden_state = residual.astype(jnp.float32) + projected
    squares = lax.psum(jnp.sum(hidden_state * hidden_state, axis=1), "batch")
    inverse = lax.rsqrt(squares / D + NORM_EPS)
    normed = (hidden_state * inverse[:, None] * norm_gain[None, :]).astype(jnp.bfloat16)
    token_count, top_count = expert_ids.shape
    capacity = 2 * token_count * top_count // EXPERTS
    pair_local = gate_up_weight.shape[0]
    flat_ids = expert_ids.reshape(-1)
    one_hot = (flat_ids[:, None] == jnp.arange(EXPERTS, dtype=jnp.int32)[None, :]).astype(jnp.int32)
    earlier = jnp.cumsum(one_hot, axis=0) - one_hot
    rank_in = jnp.sum(earlier * one_hot, axis=1)
    sub_half = lax.axis_index("head") // (head_size // 2)
    pair_first = lax.axis_index("sect") * (batch_size * pair_local)
    local_pair = flat_ids // 2 - pair_first
    in_sect = (local_pair >= 0) & (local_pair < batch_size * pair_local)
    full_slot = (
        (local_pair // pair_local * 2 + flat_ids % 2) * pair_local + local_pair % pair_local
    ) * capacity + rank_in
    full_slot = jnp.where(in_sect, full_slot, -1)
    slot_dev = pair_local * capacity
    slot_total = batch_size * 2 * slot_dev
    send_count = batch_size * slot_dev
    matches = (
        full_slot.reshape(token_count, top_count)[None, :, :]
        == jnp.arange(slot_total, dtype=jnp.int32)[:, None, None]
    )
    selector_full = (
        jnp.any(matches, axis=2).astype(jnp.bfloat16).reshape(batch_size, 2, slot_dev, token_count)
    )
    selector = lax.dynamic_index_in_dim(selector_full, sub_half, 1, keepdims=False).reshape(
        send_count, token_count
    )
    coefficient = route_weight / jnp.sum(route_weight, axis=1, keepdims=True)
    combine_full = jnp.sum(jnp.where(matches, coefficient[None, :, :], 0.0), axis=2).T
    cols_dev = normed.shape[1]
    outgoing = jnp.dot(selector, normed, preferred_element_type=jnp.float32).astype(jnp.bfloat16)
    outgoing = outgoing.reshape(batch_size, pair_local, capacity, cols_dev)
    arrived = lax.all_to_all(outgoing, "batch", split_axis=0, concat_axis=3, tiled=True)[0]
    mixture = jnp.einsum(
        "ecd,edgf->ecgf", arrived, gate_up_weight, preferred_element_type=jnp.float32
    )
    activated = (jax.nn.silu(mixture[:, :, 0]) * mixture[:, :, 1]).astype(jnp.bfloat16)
    expert_part = jnp.einsum(
        "ecf,efd->ecd", activated, down_weight, preferred_element_type=jnp.float32
    )
    leaving = expert_part.reshape(1, slot_dev, batch_size, cols_dev)
    came_back = (
        lax.all_to_all(
            leaving.astype(jnp.bfloat16), "batch", split_axis=2, concat_axis=0, tiled=True
        )
        .astype(leaving.dtype)
        .reshape(send_count, cols_dev)
    )
    weights_used = lax.dynamic_index_in_dim(
        combine_full.reshape(token_count, batch_size, 2, slot_dev), sub_half, 2, keepdims=False
    )
    weights_used = weights_used.reshape(token_count, send_count)
    combined = jnp.dot(weights_used, came_back, preferred_element_type=jnp.float32)
    expert_mix = lax.psum(combined, ("sect", "head"))
    return (hidden_state + expert_mix).astype(jnp.bfloat16)


def solution(mesh):
    placed = (
        P("batch", "head", "sect"),
        P("batch", None, None),
        P("batch", ("sect", "head"), None, None),
        P("batch"),
        P("batch", None, None),
        P(("sect", "head"), "batch"),
        P(None, "batch"),
        P("batch"),
        P(),
        P(),
        P(("sect", "batch"), None, None, "head"),
        P(("sect", "batch"), "head", None),
    )
    return jax.shard_map(
        on_device, mesh=mesh, in_specs=placed, out_specs=P(None, "batch"), check_vma=False
    )
```

```python
import math

import jax
import jax.numpy as jnp
from jax import lax
from jax.sharding import PartitionSpec as P

D = 4096
EXPERTS = 64


NEG_FILL = -1e30
NORM_EPS = 1e-06


def copy_for_each(shard, axis):
    copies = jnp.broadcast_to(shard, (lax.axis_size(axis), *shard.shape))
    return lax.all_to_all(copies, axis, split_axis=0, concat_axis=0, tiled=True)


def in_order(pieces, dim):
    lengths = list(pieces.shape[1:])
    lengths[dim] *= pieces.shape[0]
    return jnp.moveaxis(pieces, 0, dim).reshape(lengths)


def gathered_copies(shard, axis, dim):
    pieces = copy_for_each(shard, axis)
    return in_order(pieces, dim)


def from_partner(shard, axis, distance):
    return lax.ppermute(shard, axis, [(i, i ^ 1 << distance) for i in range(lax.axis_size(axis))])


def taken_together(shard, axis):
    return copy_for_each(shard, axis).astype(jnp.float32).sum(axis=0)


def of_everyone(shard, axis):
    return copy_for_each(shard, axis).sum(axis=0)


def merge_pair(first, second):
    first_max, first_sum, first_acc = first
    second_max, second_sum, second_acc = second
    joined = jnp.maximum(first_max, second_max)
    first_factor = jnp.exp(first_max - joined)
    second_factor = jnp.exp(second_max - joined)
    return (
        joined,
        first_sum * first_factor + second_sum * second_factor,
        first_acc * first_factor[..., None] + second_acc * second_factor[..., None],
    )


def merge_packed(first, second, width):
    first_max, first_sum = first[..., width], first[..., width + 1]
    second_max, second_sum = second[..., width], second[..., width + 1]
    joined = jnp.maximum(first_max, second_max)
    first_factor = jnp.exp(first_max - joined)
    second_factor = jnp.exp(second_max - joined)
    return jnp.concatenate(
        [
            first[..., :width] * first_factor[..., None] + second[..., :width] * second_factor[..., None],
            joined[..., None],
            (first_sum * first_factor + second_sum * second_factor)[..., None],
        ],
        axis=2,
    )


def head_slice(partial_value, begin_at, span_size):
    return tuple(
        (lax.dynamic_slice_in_dim(member, begin_at, span_size, 1) for member in partial_value)
    )


def on_device(
    queries,
    newest_key_value,
    page_cache,
    lengths,
    page_ids,
    out_weight,
    residual,
    norm_gain,
    expert_ids,
    route_weight,
    gate_up_weight,
    down_weight,
):
    seq_count = queries.shape[0]
    head_dim = newest_key_value.shape[2] // 2
    kv_heads = newest_key_value.shape[1]
    sect_size = lax.axis_size("sect")
    head_size = lax.axis_size("head")
    batch_size = lax.axis_size("batch")
    group_size = sect_size * head_size // kv_heads
    position = lax.axis_index("sect") * head_size + lax.axis_index("head")
    kv_index = position // group_size
    quarter = position % group_size
    local_pages = page_cache.shape[1]
    page_len = page_cache.shape[2]
    scaling = 1.0 / math.sqrt(head_dim)
    kv_per_sect = kv_heads // sect_size
    per_target = [
        queries[..., (target * kv_per_sect // head_size) * head_dim :][..., :head_dim]
        for target in range(head_size)
    ]
    group_query = in_order(
        lax.all_to_all(jnp.stack(per_target), "head", split_axis=0, concat_axis=0, tiled=True), 1
    )
    heads_dev = group_query.shape[1] // group_size
    block_cols = heads_dev * head_dim
    chosen = lax.dynamic_index_in_dim(page_ids, kv_index, 1, keepdims=False)
    leading_page = quarter * local_pages
    page_number = jnp.broadcast_to(
        leading_page + jnp.arange(local_pages, dtype=jnp.int32), (seq_count, local_pages)
    )
    page_used = jnp.any(chosen[:, :, None] == page_number[:, None, :], axis=1)
    token_place = (
        page_number[:, :, None] * page_len + jnp.arange(page_len, dtype=jnp.int32)[None, None, :]
    )
    key_count = page_cache.shape[1] * page_len
    usable_pages = (page_used[:, :, None] & (token_place < lengths[:, None, None])).reshape(
        seq_count, key_count
    )
    gathered_keys = page_cache[..., :head_dim].reshape(seq_count, key_count, head_dim)
    gathered_values = page_cache[..., head_dim:].reshape(seq_count, key_count, head_dim)
    scores = (
        jnp.einsum("shd,skd->shk", group_query, gathered_keys, preferred_element_type=jnp.float32)
        * scaling
    )
    scores = jnp.where(usable_pages[:, None, :], scores, NEG_FILL)
    newest_entry = lax.dynamic_index_in_dim(newest_key_value, kv_index, 1, keepdims=False)
    fresh_score = (
        jnp.einsum(
            "shd,sd->sh",
            group_query,
            newest_entry[:, :head_dim],
            preferred_element_type=jnp.float32,
        )
        * scaling
    )
    leading = quarter == 0
    fresh_score = jnp.where(leading, fresh_score, NEG_FILL)
    running_max = jnp.maximum(jnp.max(scores, axis=2), fresh_score)
    weights = jnp.where(usable_pages[:, None, :], jnp.exp(scores - running_max[..., None]), 0.0)
    fresh_weight = jnp.where(leading, jnp.exp(fresh_score - running_max), 0.0)
    running_sum = jnp.sum(weights, axis=2) + fresh_weight
    weighted = jnp.einsum(
        "shk,skd->shd",
        weights.astype(jnp.bfloat16),
        gathered_values,
        preferred_element_type=jnp.float32,
    )
    weighted = weighted + fresh_weight.astype(jnp.bfloat16).astype(jnp.float32)[
        ..., None
    ] * newest_entry[:, None, head_dim:].astype(jnp.float32)
    packed = jnp.concatenate([weighted, running_max[..., None], running_sum[..., None]], axis=2)
    bit_count = group_size.bit_length() - 1
    for bit_index in reversed(range(bit_count)):
        half_heads = packed.shape[1] // 2
        keep_half = quarter >> bit_index & 1
        kept = lax.dynamic_slice_in_dim(packed, keep_half * half_heads, half_heads, 1)
        sent = lax.dynamic_slice_in_dim(packed, (1 - keep_half) * half_heads, half_heads, 1)
        partner = from_partner(sent, "head", bit_index)
        packed = merge_packed(kept, partner, head_dim)
    attention = (
        (packed[..., :head_dim] / packed[..., head_dim + 1 :])
        .reshape(seq_count, block_cols)
        .astype(jnp.bfloat16)
    )
    cols_dev = residual.shape[1]
    gain_row = jnp.zeros((1, block_cols), jnp.float32).at[0, :cols_dev].set(norm_gain)
    carried = gathered_copies(
        jnp.concatenate([attention.astype(jnp.float32), gain_row], axis=0), "batch", 0
    ).reshape(lax.axis_size("batch"), seq_count + 1, block_cols)
    all_attention = carried[:, :seq_count].reshape(-1, block_cols).astype(jnp.bfloat16)
    full_gain = carried[:, seq_count, :cols_dev].reshape(-1)
    head_terms = jnp.dot(all_attention, out_weight, preferred_element_type=jnp.float32)
    projected = taken_together(head_terms.astype(jnp.bfloat16), ("sect", "head")).astype(
        jnp.float32
    )
    hidden_state = residual.astype(jnp.float32) + projected
    token_count, top_count = expert_ids.shape
    capacity = 2 * token_count * top_count // EXPERTS
    pair_local = gate_up_weight.shape[0]
    flat_ids = expert_ids.reshape(-1)
    one_hot = (flat_ids[:, None] == jnp.arange(EXPERTS, dtype=jnp.int32)[None, :]).astype(jnp.int32)
    earlier = jnp.cumsum(one_hot, axis=0) - one_hot
    rank_in = jnp.sum(earlier * one_hot, axis=1)
    sub_half = lax.axis_index("head") // (head_size // 2)
    pair_first = lax.axis_index("sect") * (batch_size * pair_local)
    local_pair = flat_ids // 2 - pair_first
    in_sect = (local_pair >= 0) & (local_pair < batch_size * pair_local)
    full_slot = (
        (local_pair // pair_local * 2 + flat_ids % 2) * pair_local + local_pair % pair_local
    ) * capacity + rank_in
    full_slot = jnp.where(in_sect, full_slot, -1)
    slot_dev = pair_local * capacity
    slot_total = batch_size * 2 * slot_dev
    send_count = batch_size * slot_dev
    matches = (
        full_slot.reshape(token_count, top_count)[None, :, :]
        == jnp.arange(slot_total, dtype=jnp.int32)[:, None, None]
    )
    selector_full = (
        jnp.any(matches, axis=2).astype(jnp.float32).reshape(batch_size, 2, slot_dev, token_count)
    )
    selector = lax.dynamic_index_in_dim(selector_full, sub_half, 1, keepdims=False).reshape(
        send_count, token_count
    )
    coefficient = route_weight / jnp.sum(route_weight, axis=1, keepdims=True)
    combine_full = jnp.sum(jnp.where(matches, coefficient[None, :, :], 0.0), axis=2).T
    outgoing = jnp.dot(
        selector, hidden_state, precision=lax.Precision.HIGHEST, preferred_element_type=jnp.float32
    )
    outgoing = outgoing.reshape(batch_size, pair_local, capacity, cols_dev)
    rows = lax.all_to_all(outgoing, "batch", split_axis=0, concat_axis=3, tiled=True)[0]
    squares = jnp.sum(rows * rows, axis=2)
    inverse = lax.rsqrt(squares / D + NORM_EPS)
    arrived = (rows * inverse[..., None] * full_gain[None, None, :]).astype(jnp.bfloat16)
    mixture = jnp.einsum(
        "ecd,edgf->ecgf", arrived, gate_up_weight, preferred_element_type=jnp.float32
    )
    activated = (jax.nn.silu(mixture[:, :, 0]) * mixture[:, :, 1]).astype(jnp.bfloat16)
    expert_part = jnp.einsum(
        "ecf,efd->ecd", activated, down_weight, preferred_element_type=jnp.float32
    )
    leaving = expert_part.reshape(1, slot_dev, batch_size, cols_dev)
    came_back = (
        lax.all_to_all(
            leaving.astype(jnp.bfloat16), "batch", split_axis=2, concat_axis=0, tiled=True
        )
        .astype(leaving.dtype)
        .reshape(send_count, cols_dev)
    )
    weights_used = lax.dynamic_index_in_dim(
        combine_full.reshape(token_count, batch_size, 2, slot_dev), sub_half, 2, keepdims=False
    )
    weights_used = weights_used.reshape(token_count, send_count)
    combined = jnp.dot(weights_used, came_back, preferred_element_type=jnp.float32)
    expert_mix = taken_together(combined.astype(jnp.bfloat16), ("sect", "head")).astype(jnp.float32)
    return (hidden_state + expert_mix).astype(jnp.bfloat16)


def solution(mesh):
    placed = (
        P("batch", "head", "sect"),
        P("batch", None, None),
        P("batch", ("sect", "head"), None, None),
        P("batch"),
        P("batch", None, None),
        P(("sect", "head"), "batch"),
        P(None, "batch"),
        P("batch"),
        P(),
        P(),
        P(("sect", "batch"), None, None, "head"),
        P(("sect", "batch"), "head", None),
    )
    return jax.shard_map(
        on_device, mesh=mesh, in_specs=placed, out_specs=P(None, "batch"), check_vma=False
    )
```

```python
import math

import jax
import jax.numpy as jnp
from jax import lax
from jax.sharding import PartitionSpec as P

D = 4096
EXPERTS = 64


NEG_FILL = -1e30
NORM_EPS = 1e-06


def copy_for_each(shard, axis):
    copies = jnp.broadcast_to(shard, (lax.axis_size(axis), *shard.shape))
    return lax.all_to_all(copies, axis, split_axis=0, concat_axis=0, tiled=True)


def in_order(pieces, dim):
    lengths = list(pieces.shape[1:])
    lengths[dim] *= pieces.shape[0]
    return jnp.moveaxis(pieces, 0, dim).reshape(lengths)


def gathered_copies(shard, axis, dim):
    pieces = copy_for_each(shard, axis)
    return in_order(pieces, dim)


def from_partner(shard, axis, distance):
    return lax.ppermute(shard, axis, [(i, i ^ 1 << distance) for i in range(lax.axis_size(axis))])


def taken_together(shard, axis):
    return copy_for_each(shard, axis).astype(jnp.float32).sum(axis=0)


def of_everyone(shard, axis):
    return copy_for_each(shard, axis).sum(axis=0)


def merge_pair(first, second):
    first_max, first_sum, first_acc = first
    second_max, second_sum, second_acc = second
    joined = jnp.maximum(first_max, second_max)
    first_factor = jnp.exp(first_max - joined)
    second_factor = jnp.exp(second_max - joined)
    return (
        joined,
        first_sum * first_factor + second_sum * second_factor,
        first_acc * first_factor[..., None] + second_acc * second_factor[..., None],
    )


def split_three(value):
    high = lax.reduce_precision(value, exponent_bits=8, mantissa_bits=7)
    rest = value - high
    middle = lax.reduce_precision(rest, exponent_bits=8, mantissa_bits=7)
    low = rest - middle
    return jnp.stack([high, middle, low]).astype(jnp.bfloat16)


def join_three(parts):
    parts = parts.astype(jnp.float32)
    return (parts[:, 0] + parts[:, 1] + parts[:, 2]).reshape(-1)


def merge_packed(first, second, width):
    first_max, first_sum = first[..., width], first[..., width + 1]
    second_max, second_sum = second[..., width], second[..., width + 1]
    joined = jnp.maximum(first_max, second_max)
    first_factor = jnp.exp(first_max - joined)
    second_factor = jnp.exp(second_max - joined)
    return jnp.concatenate(
        [
            first[..., :width] * first_factor[..., None] + second[..., :width] * second_factor[..., None],
            joined[..., None],
            (first_sum * first_factor + second_sum * second_factor)[..., None],
        ],
        axis=2,
    )


def head_slice(partial_value, begin_at, span_size):
    return tuple(
        (lax.dynamic_slice_in_dim(member, begin_at, span_size, 1) for member in partial_value)
    )


def on_device(
    queries,
    newest_key_value,
    page_cache,
    lengths,
    page_ids,
    out_weight,
    residual,
    norm_gain,
    expert_ids,
    route_weight,
    gate_up_weight,
    down_weight,
):
    seq_count = queries.shape[0]
    head_dim = newest_key_value.shape[2] // 2
    kv_heads = newest_key_value.shape[1]
    sect_size = lax.axis_size("sect")
    head_size = lax.axis_size("head")
    batch_size = lax.axis_size("batch")
    group_size = sect_size * head_size // kv_heads
    position = lax.axis_index("sect") * head_size + lax.axis_index("head")
    kv_index = position // group_size
    quarter = position % group_size
    local_pages = page_cache.shape[1]
    page_len = page_cache.shape[2]
    scaling = 1.0 / math.sqrt(head_dim)
    kv_per_sect = kv_heads // sect_size
    by_kv = jnp.moveaxis(queries.reshape(*queries.shape[:2], kv_per_sect, head_dim), 2, 0)
    per_target = jnp.broadcast_to(
        by_kv[:, None], (kv_per_sect, head_size // kv_per_sect, *by_kv.shape[1:])
    ).reshape(head_size, *by_kv.shape[1:])
    group_query = in_order(
        lax.all_to_all(per_target, "head", split_axis=0, concat_axis=0, tiled=True), 1
    )
    heads_dev = group_query.shape[1] // group_size
    block_cols = heads_dev * head_dim
    chosen = lax.dynamic_index_in_dim(page_ids, kv_index, 1, keepdims=False)
    leading_page = quarter * local_pages
    page_number = jnp.broadcast_to(
        leading_page + jnp.arange(local_pages, dtype=jnp.int32), (seq_count, local_pages)
    )
    page_used = jnp.any(chosen[:, :, None] == page_number[:, None, :], axis=1)
    token_place = (
        page_number[:, :, None] * page_len + jnp.arange(page_len, dtype=jnp.int32)[None, None, :]
    )
    key_count = page_cache.shape[1] * page_len
    usable_pages = (page_used[:, :, None] & (token_place < lengths[:, None, None])).reshape(
        seq_count, key_count
    )
    gathered_keys = page_cache[..., :head_dim].reshape(seq_count, key_count, head_dim)
    gathered_values = page_cache[..., head_dim:].reshape(seq_count, key_count, head_dim)
    scores = (
        jnp.einsum("shd,skd->shk", group_query, gathered_keys, preferred_element_type=jnp.float32)
        * scaling
    )
    scores = jnp.where(usable_pages[:, None, :], scores, NEG_FILL)
    newest_entry = lax.dynamic_index_in_dim(newest_key_value, kv_index, 1, keepdims=False)
    fresh_score = (
        jnp.einsum(
            "shd,sd->sh",
            group_query,
            newest_entry[:, :head_dim],
            preferred_element_type=jnp.float32,
        )
        * scaling
    )
    leading = quarter == 0
    fresh_score = jnp.where(leading, fresh_score, NEG_FILL)
    running_max = jnp.maximum(jnp.max(scores, axis=2), fresh_score)
    weights = jnp.where(usable_pages[:, None, :], jnp.exp(scores - running_max[..., None]), 0.0)
    fresh_weight = jnp.where(leading, jnp.exp(fresh_score - running_max), 0.0)
    running_sum = jnp.sum(weights, axis=2) + fresh_weight
    weighted = jnp.einsum(
        "shk,skd->shd",
        weights.astype(jnp.bfloat16),
        gathered_values,
        preferred_element_type=jnp.float32,
    )
    weighted = weighted + fresh_weight.astype(jnp.bfloat16).astype(jnp.float32)[
        ..., None
    ] * newest_entry[:, None, head_dim:].astype(jnp.float32)
    packed = jnp.concatenate([weighted, running_max[..., None], running_sum[..., None]], axis=2)
    bit_count = group_size.bit_length() - 1
    for bit_index in reversed(range(bit_count)):
        half_heads = packed.shape[1] // 2
        keep_half = quarter >> bit_index & 1
        kept = lax.dynamic_slice_in_dim(packed, keep_half * half_heads, half_heads, 1)
        sent = lax.dynamic_slice_in_dim(packed, (1 - keep_half) * half_heads, half_heads, 1)
        partner = from_partner(sent, "head", bit_index)
        packed = merge_packed(kept, partner, head_dim)
    attention = (
        (packed[..., :head_dim] / packed[..., head_dim + 1 :])
        .reshape(seq_count, block_cols)
        .astype(jnp.bfloat16)
    )
    cols_dev = residual.shape[1]
    gain_parts = split_three(norm_gain)
    gain_rows = -(-gain_parts.size // block_cols)
    gain_block = jnp.pad(gain_parts.reshape(-1), (0, gain_rows * block_cols - gain_parts.size))
    carried = gathered_copies(
        jnp.concatenate([attention, gain_block.reshape(gain_rows, block_cols)], axis=0), "batch", 0
    ).reshape(lax.axis_size("batch"), seq_count + gain_rows, block_cols)
    all_attention = carried[:, :seq_count].reshape(-1, block_cols)
    got_parts = carried[:, seq_count:].reshape(lax.axis_size("batch"), -1)[:, : gain_parts.size]
    full_gain = join_three(got_parts.reshape(-1, 3, cols_dev))
    head_terms = jnp.dot(all_attention, out_weight, preferred_element_type=jnp.float32)
    projected = taken_together(head_terms.astype(jnp.bfloat16), ("sect", "head")).astype(
        jnp.float32
    )
    hidden_state = residual.astype(jnp.float32) + projected
    token_count, top_count = expert_ids.shape
    capacity = 2 * token_count * top_count // EXPERTS
    pair_local = gate_up_weight.shape[0]
    flat_ids = expert_ids.reshape(-1)
    one_hot = (flat_ids[:, None] == jnp.arange(EXPERTS, dtype=jnp.int32)[None, :]).astype(jnp.int32)
    earlier = jnp.cumsum(one_hot, axis=0) - one_hot
    rank_in = jnp.sum(earlier * one_hot, axis=1)
    sub_half = lax.axis_index("head") // (head_size // 2)
    pair_first = lax.axis_index("sect") * (batch_size * pair_local)
    local_pair = flat_ids // 2 - pair_first
    in_sect = (local_pair >= 0) & (local_pair < batch_size * pair_local)
    full_slot = (
        (local_pair // pair_local * 2 + flat_ids % 2) * pair_local + local_pair % pair_local
    ) * capacity + rank_in
    full_slot = jnp.where(in_sect, full_slot, -1)
    slot_dev = pair_local * capacity
    slot_total = batch_size * 2 * slot_dev
    send_count = batch_size * slot_dev
    matches = (
        full_slot.reshape(token_count, top_count)[None, :, :]
        == jnp.arange(slot_total, dtype=jnp.int32)[:, None, None]
    )
    selector_full = (
        jnp.any(matches, axis=2).astype(jnp.bfloat16).reshape(batch_size, 2, slot_dev, token_count)
    )
    selector = lax.dynamic_index_in_dim(selector_full, sub_half, 1, keepdims=False).reshape(
        send_count, token_count
    )
    coefficient = route_weight / jnp.sum(route_weight, axis=1, keepdims=True)
    combine_full = jnp.sum(jnp.where(matches, coefficient[None, :, :], 0.0), axis=2).T
    outgoing = jnp.dot(
        selector, hidden_state.astype(jnp.bfloat16), preferred_element_type=jnp.float32
    ).astype(jnp.bfloat16)
    outgoing = outgoing.reshape(batch_size, pair_local, capacity, cols_dev)
    rows = lax.all_to_all(outgoing, "batch", split_axis=0, concat_axis=3, tiled=True)[0]
    rows = rows.astype(jnp.float32)
    squares = jnp.sum(rows * rows, axis=2)
    inverse = lax.rsqrt(squares / D + NORM_EPS)
    arrived = (rows * inverse[..., None] * full_gain[None, None, :]).astype(jnp.bfloat16)
    mixture = jnp.einsum(
        "ecd,edgf->ecgf", arrived, gate_up_weight, preferred_element_type=jnp.float32
    )
    activated = (jax.nn.silu(mixture[:, :, 0]) * mixture[:, :, 1]).astype(jnp.bfloat16)
    expert_part = jnp.einsum(
        "ecf,efd->ecd", activated, down_weight, preferred_element_type=jnp.float32
    )
    leaving = expert_part.reshape(1, slot_dev, batch_size, cols_dev)
    came_back = (
        lax.all_to_all(
            leaving.astype(jnp.bfloat16), "batch", split_axis=2, concat_axis=0, tiled=True
        )
        .astype(leaving.dtype)
        .reshape(send_count, cols_dev)
    )
    weights_used = lax.dynamic_index_in_dim(
        combine_full.reshape(token_count, batch_size, 2, slot_dev), sub_half, 2, keepdims=False
    )
    weights_used = weights_used.reshape(token_count, send_count)
    combined = jnp.dot(weights_used, came_back, preferred_element_type=jnp.float32)
    expert_mix = taken_together(combined.astype(jnp.bfloat16), ("sect", "head")).astype(jnp.float32)
    return (hidden_state + expert_mix).astype(jnp.bfloat16)


def solution(mesh):
    placed = (
        P("batch", "head", "sect"),
        P("batch", None, None),
        P("batch", ("sect", "head"), None, None),
        P("batch"),
        P("batch", None, None),
        P(("sect", "head"), "batch"),
        P(None, "batch"),
        P("batch"),
        P(),
        P(),
        P(("sect", "batch"), None, None, "head"),
        P(("sect", "batch"), "head", None),
    )
    return jax.shard_map(
        on_device, mesh=mesh, in_specs=placed, out_specs=P(None, "batch"), check_vma=False
    )
```

```python
import math

import jax
import jax.numpy as jnp
from jax import lax
from jax.sharding import PartitionSpec as P

D = 4096
EXPERTS = 64


NEG_FILL = -1e30
NORM_EPS = 1e-06


def copy_for_each(shard, axis):
    copies = jnp.broadcast_to(shard, (lax.axis_size(axis), *shard.shape))
    return lax.all_to_all(copies, axis, split_axis=0, concat_axis=0, tiled=True)


def in_order(pieces, dim):
    lengths = list(pieces.shape[1:])
    lengths[dim] *= pieces.shape[0]
    return jnp.moveaxis(pieces, 0, dim).reshape(lengths)


def gathered_copies(shard, axis, dim):
    pieces = copy_for_each(shard, axis)
    return in_order(pieces, dim)


def from_partner(shard, axis, distance):
    return lax.ppermute(shard, axis, [(i, i ^ 1 << distance) for i in range(lax.axis_size(axis))])


def taken_together(shard, axis):
    return copy_for_each(shard, axis).astype(jnp.float32).sum(axis=0)


def of_everyone(shard, axis):
    return copy_for_each(shard, axis).sum(axis=0)


def merge_pair(first, second):
    first_max, first_sum, first_acc = first
    second_max, second_sum, second_acc = second
    joined = jnp.maximum(first_max, second_max)
    first_factor = jnp.exp(first_max - joined)
    second_factor = jnp.exp(second_max - joined)
    return (
        joined,
        first_sum * first_factor + second_sum * second_factor,
        first_acc * first_factor[..., None] + second_acc * second_factor[..., None],
    )


def split_three(value):
    high = lax.reduce_precision(value, exponent_bits=8, mantissa_bits=7)
    rest = value - high
    middle = lax.reduce_precision(rest, exponent_bits=8, mantissa_bits=7)
    low = rest - middle
    return jnp.stack([high, middle, low]).astype(jnp.bfloat16)


def merge_packed(first, second, width):
    first_max, first_sum = first[..., width], first[..., width + 1]
    second_max, second_sum = second[..., width], second[..., width + 1]
    joined = jnp.maximum(first_max, second_max)
    first_factor = jnp.exp(first_max - joined)
    second_factor = jnp.exp(second_max - joined)
    return jnp.concatenate(
        [
            first[..., :width] * first_factor[..., None] + second[..., :width] * second_factor[..., None],
            joined[..., None],
            (first_sum * first_factor + second_sum * second_factor)[..., None],
        ],
        axis=2,
    )


def head_slice(partial_value, begin_at, span_size):
    return tuple(
        (lax.dynamic_slice_in_dim(member, begin_at, span_size, 1) for member in partial_value)
    )


def on_device(
    queries,
    newest_key_value,
    page_cache,
    lengths,
    page_ids,
    out_weight,
    residual,
    norm_gain,
    expert_ids,
    route_weight,
    gate_up_weight,
    down_weight,
):
    seq_count = queries.shape[0]
    head_dim = newest_key_value.shape[2] // 2
    kv_heads = newest_key_value.shape[1]
    sect_size = lax.axis_size("sect")
    head_size = lax.axis_size("head")
    batch_size = lax.axis_size("batch")
    group_size = sect_size * head_size // kv_heads
    position = lax.axis_index("sect") * head_size + lax.axis_index("head")
    kv_index = position // group_size
    quarter = position % group_size
    local_pages = page_cache.shape[1]
    page_len = page_cache.shape[2]
    scaling = 1.0 / math.sqrt(head_dim)
    kv_per_sect = kv_heads // sect_size
    by_kv = jnp.moveaxis(queries.reshape(*queries.shape[:2], kv_per_sect, head_dim), 2, 0)
    per_target = jnp.broadcast_to(
        by_kv[:, None], (kv_per_sect, head_size // kv_per_sect, *by_kv.shape[1:])
    ).reshape(head_size, *by_kv.shape[1:])
    group_query = in_order(
        lax.all_to_all(per_target, "head", split_axis=0, concat_axis=0, tiled=True), 1
    )
    heads_dev = group_query.shape[1] // group_size
    block_cols = heads_dev * head_dim
    chosen = lax.dynamic_index_in_dim(page_ids, kv_index, 1, keepdims=False)
    leading_page = quarter * local_pages
    page_number = jnp.broadcast_to(
        leading_page + jnp.arange(local_pages, dtype=jnp.int32), (seq_count, local_pages)
    )
    page_used = jnp.any(chosen[:, :, None] == page_number[:, None, :], axis=1)
    token_place = (
        page_number[:, :, None] * page_len + jnp.arange(page_len, dtype=jnp.int32)[None, None, :]
    )
    key_count = page_cache.shape[1] * page_len
    usable_pages = (page_used[:, :, None] & (token_place < lengths[:, None, None])).reshape(
        seq_count, key_count
    )
    gathered_keys = page_cache[..., :head_dim].reshape(seq_count, key_count, head_dim)
    gathered_values = page_cache[..., head_dim:].reshape(seq_count, key_count, head_dim)
    scores = (
        jnp.einsum("shd,skd->shk", group_query, gathered_keys, preferred_element_type=jnp.float32)
        * scaling
    )
    scores = jnp.where(usable_pages[:, None, :], scores, NEG_FILL)
    newest_entry = lax.dynamic_index_in_dim(newest_key_value, kv_index, 1, keepdims=False)
    fresh_score = (
        jnp.einsum(
            "shd,sd->sh",
            group_query,
            newest_entry[:, :head_dim],
            preferred_element_type=jnp.float32,
        )
        * scaling
    )
    leading = quarter == 0
    fresh_score = jnp.where(leading, fresh_score, NEG_FILL)
    running_max = jnp.maximum(jnp.max(scores, axis=2), fresh_score)
    weights = jnp.where(usable_pages[:, None, :], jnp.exp(scores - running_max[..., None]), 0.0)
    fresh_weight = jnp.where(leading, jnp.exp(fresh_score - running_max), 0.0)
    running_sum = jnp.sum(weights, axis=2) + fresh_weight
    weighted = jnp.einsum(
        "shk,skd->shd",
        weights.astype(jnp.bfloat16),
        gathered_values,
        preferred_element_type=jnp.float32,
    )
    weighted = weighted + fresh_weight.astype(jnp.bfloat16).astype(jnp.float32)[
        ..., None
    ] * newest_entry[:, None, head_dim:].astype(jnp.float32)
    packed = jnp.concatenate([weighted, running_max[..., None], running_sum[..., None]], axis=2)
    bit_count = group_size.bit_length() - 1
    for bit_index in reversed(range(bit_count)):
        half_heads = packed.shape[1] // 2
        keep_half = quarter >> bit_index & 1
        kept = lax.dynamic_slice_in_dim(packed, keep_half * half_heads, half_heads, 1)
        sent = lax.dynamic_slice_in_dim(packed, (1 - keep_half) * half_heads, half_heads, 1)
        partner = from_partner(sent, "head", bit_index)
        packed = merge_packed(kept, partner, head_dim)
    attention = (
        (packed[..., :head_dim] / packed[..., head_dim + 1 :])
        .reshape(seq_count, block_cols)
        .astype(jnp.bfloat16)
    )
    cols_dev = residual.shape[1]
    all_attention = gathered_copies(attention, "batch", 0)
    head_terms = jnp.dot(all_attention, out_weight, preferred_element_type=jnp.float32)
    projected = taken_together(head_terms.astype(jnp.bfloat16), ("sect", "head")).astype(
        jnp.float32
    )
    hidden_state = residual.astype(jnp.float32) + projected
    token_count, top_count = expert_ids.shape
    capacity = 2 * token_count * top_count // EXPERTS
    pair_local = gate_up_weight.shape[0]
    flat_ids = expert_ids.reshape(-1)
    one_hot = (flat_ids[:, None] == jnp.arange(EXPERTS, dtype=jnp.int32)[None, :]).astype(jnp.int32)
    earlier = jnp.cumsum(one_hot, axis=0) - one_hot
    rank_in = jnp.sum(earlier * one_hot, axis=1)
    sub_half = lax.axis_index("head") // (head_size // 2)
    pair_first = lax.axis_index("sect") * (batch_size * pair_local)
    local_pair = flat_ids // 2 - pair_first
    in_sect = (local_pair >= 0) & (local_pair < batch_size * pair_local)
    full_slot = (
        (local_pair // pair_local * 2 + flat_ids % 2) * pair_local + local_pair % pair_local
    ) * capacity + rank_in
    full_slot = jnp.where(in_sect, full_slot, -1)
    slot_dev = pair_local * capacity
    slot_total = batch_size * 2 * slot_dev
    send_count = batch_size * slot_dev
    matches = (
        full_slot.reshape(token_count, top_count)[None, :, :]
        == jnp.arange(slot_total, dtype=jnp.int32)[:, None, None]
    )
    selector_full = (
        jnp.any(matches, axis=2).astype(jnp.bfloat16).reshape(batch_size, 2, slot_dev, token_count)
    )
    selector = lax.dynamic_index_in_dim(selector_full, sub_half, 1, keepdims=False).reshape(
        send_count, token_count
    )
    coefficient = route_weight / jnp.sum(route_weight, axis=1, keepdims=True)
    combine_full = jnp.sum(jnp.where(matches, coefficient[None, :, :], 0.0), axis=2).T
    scaled = (hidden_state * norm_gain[None, :]).astype(jnp.bfloat16)
    square_parts = split_three(jnp.sum(hidden_state * hidden_state, axis=1))
    outgoing = jnp.dot(selector, scaled, preferred_element_type=jnp.float32).astype(jnp.bfloat16)
    slot_squares = jnp.dot(selector, square_parts.T, preferred_element_type=jnp.float32)
    square_width = 3 * slot_dev
    square_rows = -(-square_width // cols_dev)
    square_block = jnp.pad(
        slot_squares.astype(jnp.bfloat16).reshape(batch_size, square_width),
        ((0, 0), (0, square_rows * cols_dev - square_width)),
    ).reshape(batch_size, square_rows, cols_dev)
    outgoing = jnp.concatenate(
        [outgoing.reshape(batch_size, slot_dev, cols_dev), square_block], axis=1
    )
    arrived = lax.all_to_all(outgoing, "batch", split_axis=0, concat_axis=0, tiled=True)
    rows = arrived[:, :slot_dev].reshape(batch_size, pair_local, capacity, cols_dev)
    got_squares = arrived[:, slot_dev:].reshape(batch_size, -1)[:, :square_width]
    squares = jnp.sum(
        got_squares.reshape(batch_size, slot_dev, 3).astype(jnp.float32), axis=(0, 2)
    )
    inverse = lax.rsqrt(squares / D + NORM_EPS).reshape(pair_local, capacity)
    mixture = jnp.einsum(
        "becd,ebdgf->ecgf",
        rows,
        gate_up_weight.reshape(pair_local, batch_size, cols_dev, *gate_up_weight.shape[2:]),
        preferred_element_type=jnp.float32,
    )
    mixture = mixture * inverse[:, :, None, None]
    activated = (jax.nn.silu(mixture[:, :, 0]) * mixture[:, :, 1]).astype(jnp.bfloat16)
    expert_part = jnp.einsum(
        "ecf,efd->ecd", activated, down_weight, preferred_element_type=jnp.float32
    )
    leaving = expert_part.reshape(1, slot_dev, batch_size, cols_dev)
    came_back = (
        lax.all_to_all(
            leaving.astype(jnp.bfloat16), "batch", split_axis=2, concat_axis=0, tiled=True
        )
        .astype(leaving.dtype)
        .reshape(send_count, cols_dev)
    )
    weights_used = lax.dynamic_index_in_dim(
        combine_full.reshape(token_count, batch_size, 2, slot_dev), sub_half, 2, keepdims=False
    )
    weights_used = weights_used.reshape(token_count, send_count)
    combined = jnp.dot(weights_used, came_back, preferred_element_type=jnp.float32)
    expert_mix = taken_together(combined.astype(jnp.bfloat16), ("sect", "head")).astype(jnp.float32)
    return (hidden_state + expert_mix).astype(jnp.bfloat16)


def solution(mesh):
    placed = (
        P("batch", "head", "sect"),
        P("batch", None, None),
        P("batch", ("sect", "head"), None, None),
        P("batch"),
        P("batch", None, None),
        P(("sect", "head"), "batch"),
        P(None, "batch"),
        P("batch"),
        P(),
        P(),
        P(("sect", "batch"), None, None, "head"),
        P(("sect", "batch"), "head", None),
    )
    return jax.shard_map(
        on_device, mesh=mesh, in_specs=placed, out_specs=P(None, "batch"), check_vma=False
    )
```

```python
import math

import jax
import jax.numpy as jnp
from jax import lax
from jax.sharding import PartitionSpec as P

D = 4096
EXPERTS = 64


NEG_FILL = -1e30
NORM_EPS = 1e-06


def copy_for_each(shard, axis):
    copies = jnp.broadcast_to(shard, (lax.axis_size(axis), *shard.shape))
    return lax.all_to_all(copies, axis, split_axis=0, concat_axis=0, tiled=True)


def in_order(pieces, dim):
    lengths = list(pieces.shape[1:])
    lengths[dim] *= pieces.shape[0]
    return jnp.moveaxis(pieces, 0, dim).reshape(lengths)


def gathered_copies(shard, axis, dim):
    pieces = copy_for_each(shard, axis)
    return in_order(pieces, dim)


def from_partner(shard, axis, distance):
    return lax.ppermute(shard, axis, [(i, i ^ 1 << distance) for i in range(lax.axis_size(axis))])


def taken_together(shard, axis):
    return copy_for_each(shard, axis).astype(jnp.float32).sum(axis=0)


def of_everyone(shard, axis):
    return copy_for_each(shard, axis).sum(axis=0)


def merge_pair(first, second):
    first_max, first_sum, first_acc = first
    second_max, second_sum, second_acc = second
    joined = jnp.maximum(first_max, second_max)
    first_factor = jnp.exp(first_max - joined)
    second_factor = jnp.exp(second_max - joined)
    return (
        joined,
        first_sum * first_factor + second_sum * second_factor,
        first_acc * first_factor[..., None] + second_acc * second_factor[..., None],
    )


def split_three(value):
    high = lax.reduce_precision(value, exponent_bits=8, mantissa_bits=7)
    rest = value - high
    middle = lax.reduce_precision(rest, exponent_bits=8, mantissa_bits=7)
    low = rest - middle
    return jnp.stack([high, middle, low]).astype(jnp.bfloat16)


def merge_packed(first, second, width):
    first_max, first_sum = first[..., width], first[..., width + 1]
    second_max, second_sum = second[..., width], second[..., width + 1]
    joined = jnp.maximum(first_max, second_max)
    first_factor = jnp.exp(first_max - joined)
    second_factor = jnp.exp(second_max - joined)
    return jnp.concatenate(
        [
            first[..., :width] * first_factor[..., None] + second[..., :width] * second_factor[..., None],
            joined[..., None],
            (first_sum * first_factor + second_sum * second_factor)[..., None],
        ],
        axis=2,
    )


def head_slice(partial_value, begin_at, span_size):
    return tuple(
        (lax.dynamic_slice_in_dim(member, begin_at, span_size, 1) for member in partial_value)
    )


def on_device(
    queries,
    newest_key_value,
    page_cache,
    lengths,
    page_ids,
    out_weight,
    residual,
    norm_gain,
    expert_ids,
    route_weight,
    gate_up_weight,
    down_weight,
):
    seq_count = queries.shape[0]
    head_dim = newest_key_value.shape[2] // 2
    kv_heads = newest_key_value.shape[1]
    sect_size = lax.axis_size("sect")
    head_size = lax.axis_size("head")
    batch_size = lax.axis_size("batch")
    group_size = sect_size * head_size // kv_heads
    position = lax.axis_index("sect") * head_size + lax.axis_index("head")
    kv_index = position // group_size
    quarter = position % group_size
    local_pages = page_cache.shape[1]
    page_len = page_cache.shape[2]
    scaling = 1.0 / math.sqrt(head_dim)
    kv_per_sect = kv_heads // sect_size
    by_kv = jnp.moveaxis(queries.reshape(*queries.shape[:2], kv_per_sect, head_dim), 2, 0)
    per_target = jnp.broadcast_to(
        by_kv[:, None], (kv_per_sect, head_size // kv_per_sect, *by_kv.shape[1:])
    ).reshape(head_size, *by_kv.shape[1:])
    group_query = in_order(
        lax.all_to_all(per_target, "head", split_axis=0, concat_axis=0, tiled=True), 1
    )
    heads_dev = group_query.shape[1] // group_size
    block_cols = heads_dev * head_dim
    chosen = lax.dynamic_index_in_dim(page_ids, kv_index, 1, keepdims=False)
    leading_page = quarter * local_pages
    page_number = jnp.broadcast_to(
        leading_page + jnp.arange(local_pages, dtype=jnp.int32), (seq_count, local_pages)
    )
    page_used = jnp.any(chosen[:, :, None] == page_number[:, None, :], axis=1)
    token_place = (
        page_number[:, :, None] * page_len + jnp.arange(page_len, dtype=jnp.int32)[None, None, :]
    )
    key_count = page_cache.shape[1] * page_len
    usable_pages = (page_used[:, :, None] & (token_place < lengths[:, None, None])).reshape(
        seq_count, key_count
    )
    gathered_keys = page_cache[..., :head_dim].reshape(seq_count, key_count, head_dim)
    gathered_values = page_cache[..., head_dim:].reshape(seq_count, key_count, head_dim)
    scores = (
        jnp.einsum("shd,skd->shk", group_query, gathered_keys, preferred_element_type=jnp.float32)
        * scaling
    )
    scores = jnp.where(usable_pages[:, None, :], scores, NEG_FILL)
    newest_entry = lax.dynamic_index_in_dim(newest_key_value, kv_index, 1, keepdims=False)
    fresh_score = (
        jnp.einsum(
            "shd,sd->sh",
            group_query,
            newest_entry[:, :head_dim],
            preferred_element_type=jnp.float32,
        )
        * scaling
    )
    leading = quarter == 0
    fresh_score = jnp.where(leading, fresh_score, NEG_FILL)
    running_max = jnp.maximum(jnp.max(scores, axis=2), fresh_score)
    weights = jnp.where(usable_pages[:, None, :], jnp.exp(scores - running_max[..., None]), 0.0)
    fresh_weight = jnp.where(leading, jnp.exp(fresh_score - running_max), 0.0)
    running_sum = jnp.sum(weights, axis=2) + fresh_weight
    weighted = jnp.einsum(
        "shk,skd->shd",
        weights.astype(jnp.bfloat16),
        gathered_values,
        preferred_element_type=jnp.float32,
    )
    weighted = weighted + fresh_weight.astype(jnp.bfloat16).astype(jnp.float32)[
        ..., None
    ] * newest_entry[:, None, head_dim:].astype(jnp.float32)
    packed = jnp.concatenate([weighted, running_max[..., None], running_sum[..., None]], axis=2)
    bit_count = group_size.bit_length() - 1
    for bit_index in reversed(range(bit_count)):
        half_heads = packed.shape[1] // 2
        keep_half = quarter >> bit_index & 1
        kept = lax.dynamic_slice_in_dim(packed, keep_half * half_heads, half_heads, 1)
        sent = lax.dynamic_slice_in_dim(packed, (1 - keep_half) * half_heads, half_heads, 1)
        partner = from_partner(sent, "head", bit_index)
        packed = merge_packed(kept, partner, head_dim)
    attention = (
        (packed[..., :head_dim] / packed[..., head_dim + 1 :])
        .reshape(seq_count, block_cols)
        .astype(jnp.bfloat16)
    )
    cols_dev = residual.shape[1]
    all_attention = gathered_copies(attention, "batch", 0)
    head_terms = jnp.dot(all_attention, out_weight, preferred_element_type=jnp.float32)
    projected = taken_together(head_terms.astype(jnp.bfloat16), ("sect", "head")).astype(
        jnp.float32
    )
    hidden_state = residual.astype(jnp.float32) + projected
    token_count, top_count = expert_ids.shape
    capacity = 2 * token_count * top_count // EXPERTS
    pair_local = gate_up_weight.shape[0]
    flat_ids = expert_ids.reshape(-1)
    one_hot = (flat_ids[:, None] == jnp.arange(EXPERTS, dtype=jnp.int32)[None, :]).astype(jnp.int32)
    earlier = jnp.cumsum(one_hot, axis=0) - one_hot
    rank_in = jnp.sum(earlier * one_hot, axis=1)
    sub_half = lax.axis_index("head") // (head_size // 2)
    pair_first = lax.axis_index("sect") * (batch_size * pair_local)
    local_pair = flat_ids // 2 - pair_first
    in_sect = (local_pair >= 0) & (local_pair < batch_size * pair_local)
    full_slot = (
        (local_pair // pair_local * 2 + flat_ids % 2) * pair_local + local_pair % pair_local
    ) * capacity + rank_in
    full_slot = jnp.where(in_sect, full_slot, -1)
    slot_dev = pair_local * capacity
    slot_total = batch_size * 2 * slot_dev
    send_count = batch_size * slot_dev
    matches = (
        full_slot.reshape(token_count, top_count)[None, :, :]
        == jnp.arange(slot_total, dtype=jnp.int32)[:, None, None]
    )
    selector_full = (
        jnp.any(matches, axis=2).astype(jnp.bfloat16).reshape(batch_size, 2, slot_dev, token_count)
    )
    selector = lax.dynamic_index_in_dim(selector_full, sub_half, 1, keepdims=False).reshape(
        send_count, token_count
    )
    coefficient = route_weight / jnp.sum(route_weight, axis=1, keepdims=True)
    combine_full = jnp.sum(jnp.where(matches, coefficient[None, :, :], 0.0), axis=2).T
    scaled = (hidden_state * norm_gain[None, :]).astype(jnp.bfloat16)
    square_parts = split_three(jnp.sum(hidden_state * hidden_state, axis=1))
    outgoing = jnp.dot(selector, scaled, preferred_element_type=jnp.float32).astype(jnp.bfloat16)
    slot_squares = jnp.dot(square_parts, selector.T, preferred_element_type=jnp.float32)
    square_width = 3 * slot_dev
    square_rows = -(-square_width // cols_dev)
    square_block = jnp.pad(
        jnp.moveaxis(slot_squares.astype(jnp.bfloat16).reshape(3, batch_size, slot_dev), 0, 1)
        .reshape(batch_size, square_width),
        ((0, 0), (0, square_rows * cols_dev - square_width)),
    ).reshape(batch_size, square_rows, cols_dev)
    outgoing = jnp.concatenate(
        [outgoing.reshape(batch_size, slot_dev, cols_dev), square_block], axis=1
    )
    arrived = lax.all_to_all(outgoing, "batch", split_axis=0, concat_axis=0, tiled=True)
    rows = arrived[:, :slot_dev].reshape(batch_size, pair_local, capacity, cols_dev)
    got_squares = arrived[:, slot_dev:].reshape(batch_size, -1)[:, :square_width]
    squares = jnp.sum(
        got_squares.reshape(batch_size * 3, slot_dev).astype(jnp.float32), axis=0
    )
    inverse = lax.rsqrt(squares / D + NORM_EPS).reshape(pair_local, capacity)
    mixture = jnp.einsum(
        "becd,ebdgf->ecgf",
        rows,
        gate_up_weight.reshape(pair_local, batch_size, cols_dev, *gate_up_weight.shape[2:]),
        preferred_element_type=jnp.float32,
    )
    mixture = mixture * inverse[:, :, None, None]
    activated = (jax.nn.silu(mixture[:, :, 0]) * mixture[:, :, 1]).astype(jnp.bfloat16)
    expert_part = jnp.einsum(
        "ecf,efd->ecd", activated, down_weight, preferred_element_type=jnp.float32
    )
    leaving = expert_part.reshape(1, slot_dev, batch_size, cols_dev)
    came_back = (
        lax.all_to_all(
            leaving.astype(jnp.bfloat16), "batch", split_axis=2, concat_axis=0, tiled=True
        )
        .astype(leaving.dtype)
        .reshape(send_count, cols_dev)
    )
    weights_used = lax.dynamic_index_in_dim(
        combine_full.reshape(token_count, batch_size, 2, slot_dev), sub_half, 2, keepdims=False
    )
    weights_used = weights_used.reshape(token_count, send_count)
    combined = jnp.dot(weights_used, came_back, preferred_element_type=jnp.float32)
    expert_mix = taken_together(combined.astype(jnp.bfloat16), ("sect", "head")).astype(jnp.float32)
    return (hidden_state + expert_mix).astype(jnp.bfloat16)


def solution(mesh):
    placed = (
        P("batch", "head", "sect"),
        P("batch", None, None),
        P("batch", ("sect", "head"), None, None),
        P("batch"),
        P("batch", None, None),
        P(("sect", "head"), "batch"),
        P(None, "batch"),
        P("batch"),
        P(),
        P(),
        P(("sect", "batch"), None, None, "head"),
        P(("sect", "batch"), "head", None),
    )
    return jax.shard_map(
        on_device, mesh=mesh, in_specs=placed, out_specs=P(None, "batch"), check_vma=False
    )
```

```python
import math

import jax
import jax.numpy as jnp
from jax import lax
from jax.sharding import PartitionSpec as P

D = 4096
EXPERTS = 64
KEY_VALUE_HEADS = 4
HEAD = ("htop", "hq")


NEG_FILL = -1e30
NORM_EPS = 1e-06


def copy_for_each(shard, axis):
    copies = jnp.broadcast_to(shard, (lax.axis_size(axis), *shard.shape))
    return lax.all_to_all(copies, axis, split_axis=0, concat_axis=0, tiled=True)


def in_order(pieces, dim):
    lengths = list(pieces.shape[1:])
    lengths[dim] *= pieces.shape[0]
    return jnp.moveaxis(pieces, 0, dim).reshape(lengths)


def gathered_copies(shard, axis, dim):
    pieces = copy_for_each(shard, axis)
    return in_order(pieces, dim)


def from_partner(shard, axis, distance):
    return lax.ppermute(shard, axis, [(i, i ^ 1 << distance) for i in range(lax.axis_size(axis))])


def taken_together(shard, axis):
    return copy_for_each(shard, axis).astype(jnp.float32).sum(axis=0)


def of_everyone(shard, axis):
    return copy_for_each(shard, axis).sum(axis=0)


def merge_pair(first, second):
    first_max, first_sum, first_acc = first
    second_max, second_sum, second_acc = second
    joined = jnp.maximum(first_max, second_max)
    first_factor = jnp.exp(first_max - joined)
    second_factor = jnp.exp(second_max - joined)
    return (
        joined,
        first_sum * first_factor + second_sum * second_factor,
        first_acc * first_factor[..., None] + second_acc * second_factor[..., None],
    )


def split_three(value):
    high = lax.reduce_precision(value, exponent_bits=8, mantissa_bits=7)
    rest = value - high
    middle = lax.reduce_precision(rest, exponent_bits=8, mantissa_bits=7)
    low = rest - middle
    return jnp.stack([high, middle, low]).astype(jnp.bfloat16)


def merge_packed(first, second, width):
    first_max, first_sum = first[..., width], first[..., width + 1]
    second_max, second_sum = second[..., width], second[..., width + 1]
    joined = jnp.maximum(first_max, second_max)
    first_factor = jnp.exp(first_max - joined)
    second_factor = jnp.exp(second_max - joined)
    return jnp.concatenate(
        [
            first[..., :width] * first_factor[..., None] + second[..., :width] * second_factor[..., None],
            joined[..., None],
            (first_sum * first_factor + second_sum * second_factor)[..., None],
        ],
        axis=2,
    )


def head_slice(partial_value, begin_at, span_size):
    return tuple(
        (lax.dynamic_slice_in_dim(member, begin_at, span_size, 1) for member in partial_value)
    )


def on_device(
    queries,
    newest_key_value,
    page_cache,
    lengths,
    page_ids,
    out_weight,
    residual,
    norm_gain,
    expert_ids,
    route_weight,
    gate_up_weight,
    down_weight,
):
    seq_count = queries.shape[0]
    head_dim = newest_key_value.shape[2] // 2
    kv_heads = newest_key_value.shape[1]
    sect_size = lax.axis_size("sect")
    head_size = lax.axis_size(HEAD)
    batch_size = lax.axis_size("batch")
    group_size = sect_size * head_size // kv_heads
    position = lax.axis_index("sect") * head_size + lax.axis_index(HEAD)
    kv_index = position // group_size
    quarter = position % group_size
    local_pages = page_cache.shape[1]
    page_len = page_cache.shape[2]
    scaling = 1.0 / math.sqrt(head_dim)
    kv_per_sect = kv_heads // sect_size
    by_kv = jnp.moveaxis(queries.reshape(*queries.shape[:2], kv_per_sect, head_dim), 2, 0)
    per_target = jnp.broadcast_to(
        by_kv[:, None], (kv_per_sect, head_size // kv_per_sect, *by_kv.shape[1:])
    ).reshape(head_size, *by_kv.shape[1:])
    group_query = in_order(
        lax.all_to_all(per_target, HEAD, split_axis=0, concat_axis=0, tiled=True), 1
    )
    heads_dev = group_query.shape[1] // group_size
    block_cols = heads_dev * head_dim
    chosen = lax.dynamic_index_in_dim(page_ids, kv_index, 1, keepdims=False)
    leading_page = quarter * local_pages
    page_number = jnp.broadcast_to(
        leading_page + jnp.arange(local_pages, dtype=jnp.int32), (seq_count, local_pages)
    )
    page_used = jnp.any(chosen[:, :, None] == page_number[:, None, :], axis=1)
    token_place = (
        page_number[:, :, None] * page_len + jnp.arange(page_len, dtype=jnp.int32)[None, None, :]
    )
    key_count = page_cache.shape[1] * page_len
    usable_pages = (page_used[:, :, None] & (token_place < lengths[:, None, None])).reshape(
        seq_count, key_count
    )
    gathered_keys = page_cache[..., :head_dim].reshape(seq_count, key_count, head_dim)
    gathered_values = page_cache[..., head_dim:].reshape(seq_count, key_count, head_dim)
    scores = (
        jnp.einsum("shd,skd->shk", group_query, gathered_keys, preferred_element_type=jnp.float32)
        * scaling
    )
    scores = jnp.where(usable_pages[:, None, :], scores, NEG_FILL)
    newest_entry = lax.dynamic_index_in_dim(newest_key_value, kv_index, 1, keepdims=False)
    fresh_score = (
        jnp.einsum(
            "shd,sd->sh",
            group_query,
            newest_entry[:, :head_dim],
            preferred_element_type=jnp.float32,
        )
        * scaling
    )
    leading = quarter == 0
    fresh_score = jnp.where(leading, fresh_score, NEG_FILL)
    running_max = jnp.maximum(jnp.max(scores, axis=2), fresh_score)
    weights = jnp.where(usable_pages[:, None, :], jnp.exp(scores - running_max[..., None]), 0.0)
    fresh_weight = jnp.where(leading, jnp.exp(fresh_score - running_max), 0.0)
    running_sum = jnp.sum(weights, axis=2) + fresh_weight
    weighted = jnp.einsum(
        "shk,skd->shd",
        weights.astype(jnp.bfloat16),
        gathered_values,
        preferred_element_type=jnp.float32,
    )
    weighted = weighted + fresh_weight.astype(jnp.bfloat16).astype(jnp.float32)[
        ..., None
    ] * newest_entry[:, None, head_dim:].astype(jnp.float32)
    batch_count = lax.axis_size("batch")
    chunk_rows = seq_count * heads_dev
    stats = jnp.stack([running_max, running_sum])
    stats = stats.reshape(2, seq_count, group_size, heads_dev)
    stats = jnp.moveaxis(stats, 2, 0).reshape(group_size, 2, chunk_rows)
    lane_pad = -(-chunk_rows // head_dim) * head_dim
    stats = jnp.pad(stats, ((0, 0), (0, 0), (0, lane_pad - chunk_rows)))
    stat_rows = lane_pad // head_dim
    stats = stats.reshape(group_size, 2 * stat_rows, head_dim)
    parts = weighted.reshape(seq_count, group_size, heads_dev, head_dim)
    parts = jnp.moveaxis(parts, 1, 0).reshape(group_size, chunk_rows, head_dim)
    chunk = jnp.concatenate([parts, stats], axis=1)
    outgoing_parts = jnp.broadcast_to(chunk[None], (batch_count, *chunk.shape)).reshape(
        batch_count * group_size, *chunk.shape[1:]
    )
    got = lax.all_to_all(outgoing_parts, ("batch", "hq"), split_axis=0, concat_axis=0, tiled=True)
    got = got.reshape(batch_count, group_size, *chunk.shape[1:])
    got_acc = got[:, :, :chunk_rows]
    got_stats = got[:, :, chunk_rows:].reshape(batch_count, group_size, 2, lane_pad)[..., :chunk_rows]
    got_max, got_sum = got_stats[:, :, 0], got_stats[:, :, 1]
    joined = jnp.max(got_max, axis=1, keepdims=True)
    factor = jnp.exp(got_max - joined)
    total = jnp.sum(got_sum * factor, axis=1)
    merged = jnp.sum(got_acc * factor[..., None], axis=1)
    all_attention = (
        (merged / total[..., None])
        .reshape(batch_count * seq_count, block_cols)
        .astype(jnp.bfloat16)
    )
    cols_dev = residual.shape[1]
    head_terms = jnp.dot(all_attention, out_weight, preferred_element_type=jnp.float32)
    projected = taken_together(head_terms.astype(jnp.bfloat16), ("sect", *HEAD)).astype(
        jnp.float32
    )
    hidden_state = residual.astype(jnp.float32) + projected
    token_count, top_count = expert_ids.shape
    capacity = 2 * token_count * top_count // EXPERTS
    pair_local = gate_up_weight.shape[0]
    flat_ids = expert_ids.reshape(-1)
    one_hot = (flat_ids[:, None] == jnp.arange(EXPERTS, dtype=jnp.int32)[None, :]).astype(jnp.int32)
    earlier = jnp.cumsum(one_hot, axis=0) - one_hot
    rank_in = jnp.sum(earlier * one_hot, axis=1)
    sub_half = lax.axis_index(HEAD) // (head_size // 2)
    pair_first = lax.axis_index("sect") * (batch_size * pair_local)
    local_pair = flat_ids // 2 - pair_first
    in_sect = (local_pair >= 0) & (local_pair < batch_size * pair_local)
    full_slot = (
        (local_pair // pair_local * 2 + flat_ids % 2) * pair_local + local_pair % pair_local
    ) * capacity + rank_in
    full_slot = jnp.where(in_sect, full_slot, -1)
    slot_dev = pair_local * capacity
    slot_total = batch_size * 2 * slot_dev
    send_count = batch_size * slot_dev
    matches = (
        full_slot.reshape(token_count, top_count)[None, :, :]
        == jnp.arange(slot_total, dtype=jnp.int32)[:, None, None]
    )
    selector_full = (
        jnp.any(matches, axis=2).astype(jnp.bfloat16).reshape(batch_size, 2, slot_dev, token_count)
    )
    selector = lax.dynamic_index_in_dim(selector_full, sub_half, 1, keepdims=False).reshape(
        send_count, token_count
    )
    coefficient = route_weight / jnp.sum(route_weight, axis=1, keepdims=True)
    combine_full = jnp.sum(jnp.where(matches, coefficient[None, :, :], 0.0), axis=2).T
    scaled = (hidden_state * norm_gain[None, :]).astype(jnp.bfloat16)
    square_parts = split_three(jnp.sum(hidden_state * hidden_state, axis=1))
    outgoing = jnp.dot(selector, scaled, preferred_element_type=jnp.float32).astype(jnp.bfloat16)
    slot_squares = jnp.dot(square_parts, selector.T, preferred_element_type=jnp.float32)
    square_width = 3 * slot_dev
    square_rows = -(-square_width // cols_dev)
    square_block = jnp.pad(
        jnp.moveaxis(slot_squares.astype(jnp.bfloat16).reshape(3, batch_size, slot_dev), 0, 1)
        .reshape(batch_size, square_width),
        ((0, 0), (0, square_rows * cols_dev - square_width)),
    ).reshape(batch_size, square_rows, cols_dev)
    outgoing = jnp.concatenate(
        [outgoing.reshape(batch_size, slot_dev, cols_dev), square_block], axis=1
    )
    arrived = lax.all_to_all(outgoing, "batch", split_axis=0, concat_axis=0, tiled=True)
    rows = arrived[:, :slot_dev].reshape(batch_size, pair_local, capacity, cols_dev)
    got_squares = arrived[:, slot_dev:].reshape(batch_size, -1)[:, :square_width]
    squares = jnp.sum(
        got_squares.reshape(batch_size * 3, slot_dev).astype(jnp.float32), axis=0
    )
    inverse = lax.rsqrt(squares / D + NORM_EPS).reshape(pair_local, capacity)
    mixture = jnp.einsum(
        "becd,ebdgf->ecgf",
        rows,
        gate_up_weight.reshape(pair_local, batch_size, cols_dev, *gate_up_weight.shape[2:]),
        preferred_element_type=jnp.float32,
    )
    mixture = mixture * inverse[:, :, None, None]
    activated = (jax.nn.silu(mixture[:, :, 0]) * mixture[:, :, 1]).astype(jnp.bfloat16)
    expert_part = jnp.einsum(
        "ecf,efd->ecd", activated, down_weight, preferred_element_type=jnp.float32
    )
    leaving = expert_part.reshape(1, slot_dev, batch_size, cols_dev)
    came_back = (
        lax.all_to_all(
            leaving.astype(jnp.bfloat16), "batch", split_axis=2, concat_axis=0, tiled=True
        )
        .astype(leaving.dtype)
        .reshape(send_count, cols_dev)
    )
    weights_used = lax.dynamic_index_in_dim(
        combine_full.reshape(token_count, batch_size, 2, slot_dev), sub_half, 2, keepdims=False
    )
    weights_used = weights_used.reshape(token_count, send_count)
    combined = jnp.dot(weights_used, came_back, preferred_element_type=jnp.float32)
    expert_mix = taken_together(combined.astype(jnp.bfloat16), ("sect", *HEAD)).astype(jnp.float32)
    return (hidden_state + expert_mix).astype(jnp.bfloat16)


def solution(mesh):
    group = mesh.shape["sect"] * mesh.shape["head"] // KEY_VALUE_HEADS
    fine = jax.sharding.Mesh(
        mesh.devices.reshape(
            mesh.shape["sect"], mesh.shape["batch"], mesh.shape["head"] // group, group
        ),
        ("sect", "batch", *HEAD),
    )
    placed = (
        P("batch", HEAD, "sect"),
        P("batch", None, None),
        P("batch", ("sect", *HEAD), None, None),
        P("batch"),
        P("batch", None, None),
        P(("sect", *HEAD), "batch"),
        P(None, "batch"),
        P("batch"),
        P(),
        P(),
        P(("sect", "batch"), None, None, HEAD),
        P(("sect", "batch"), HEAD, None),
    )
    return jax.shard_map(
        on_device, mesh=fine, in_specs=placed, out_specs=P(None, "batch"), check_vma=False
    )
```

```python
import math

import jax
import jax.numpy as jnp
from jax import lax
from jax.sharding import PartitionSpec as P

D = 4096
EXPERTS = 64


NEG_FILL = -1e30
NORM_EPS = 1e-06


def copy_for_each(shard, axis):
    copies = jnp.broadcast_to(shard, (lax.axis_size(axis), *shard.shape))
    return lax.all_to_all(copies, axis, split_axis=0, concat_axis=0, tiled=True)


def in_order(pieces, dim):
    lengths = list(pieces.shape[1:])
    lengths[dim] *= pieces.shape[0]
    return jnp.moveaxis(pieces, 0, dim).reshape(lengths)


def gathered_copies(shard, axis, dim):
    pieces = copy_for_each(shard, axis)
    return in_order(pieces, dim)


def from_partner(shard, axis, distance):
    return lax.ppermute(shard, axis, [(i, i ^ 1 << distance) for i in range(lax.axis_size(axis))])


def taken_together(shard, axis):
    return copy_for_each(shard, axis).astype(jnp.float32).sum(axis=0)


def of_everyone(shard, axis):
    return copy_for_each(shard, axis).sum(axis=0)


def merge_pair(first, second):
    first_max, first_sum, first_acc = first
    second_max, second_sum, second_acc = second
    joined = jnp.maximum(first_max, second_max)
    first_factor = jnp.exp(first_max - joined)
    second_factor = jnp.exp(second_max - joined)
    return (
        joined,
        first_sum * first_factor + second_sum * second_factor,
        first_acc * first_factor[..., None] + second_acc * second_factor[..., None],
    )


def split_three(value):
    high = lax.reduce_precision(value, exponent_bits=8, mantissa_bits=7)
    rest = value - high
    middle = lax.reduce_precision(rest, exponent_bits=8, mantissa_bits=7)
    low = rest - middle
    return jnp.stack([high, middle, low]).astype(jnp.bfloat16)


def merge_packed(first, second, width):
    first_max, first_sum = first[..., width], first[..., width + 1]
    second_max, second_sum = second[..., width], second[..., width + 1]
    joined = jnp.maximum(first_max, second_max)
    first_factor = jnp.exp(first_max - joined)
    second_factor = jnp.exp(second_max - joined)
    return jnp.concatenate(
        [
            first[..., :width] * first_factor[..., None] + second[..., :width] * second_factor[..., None],
            joined[..., None],
            (first_sum * first_factor + second_sum * second_factor)[..., None],
        ],
        axis=2,
    )


def head_slice(partial_value, begin_at, span_size):
    return tuple(
        (lax.dynamic_slice_in_dim(member, begin_at, span_size, 1) for member in partial_value)
    )


def on_device(
    queries,
    newest_key_value,
    page_cache,
    lengths,
    page_ids,
    out_weight,
    residual,
    norm_gain,
    expert_ids,
    route_weight,
    gate_up_weight,
    down_weight,
):
    seq_count = queries.shape[0]
    head_dim = newest_key_value.shape[2] // 2
    kv_heads = newest_key_value.shape[1]
    sect_size = lax.axis_size("sect")
    head_size = lax.axis_size("head")
    batch_size = lax.axis_size("batch")
    group_size = sect_size * head_size // kv_heads
    position = lax.axis_index("sect") * head_size + lax.axis_index("head")
    kv_index = position // group_size
    quarter = position % group_size
    local_pages = page_cache.shape[1]
    page_len = page_cache.shape[2]
    scaling = 1.0 / math.sqrt(head_dim)
    kv_per_sect = kv_heads // sect_size
    by_kv = jnp.moveaxis(queries.reshape(*queries.shape[:2], kv_per_sect, head_dim), 2, 0)
    per_target = jnp.broadcast_to(
        by_kv[:, None], (kv_per_sect, head_size // kv_per_sect, *by_kv.shape[1:])
    ).reshape(head_size, *by_kv.shape[1:])
    group_query = in_order(
        lax.all_to_all(per_target, "head", split_axis=0, concat_axis=0, tiled=True), 1
    )
    heads_dev = group_query.shape[1] // group_size
    block_cols = heads_dev * head_dim
    chosen = lax.dynamic_index_in_dim(page_ids, kv_index, 1, keepdims=False)
    leading_page = quarter * local_pages
    page_number = jnp.broadcast_to(
        leading_page + jnp.arange(local_pages, dtype=jnp.int32), (seq_count, local_pages)
    )
    page_used = jnp.any(chosen[:, :, None] == page_number[:, None, :], axis=1)
    token_place = (
        page_number[:, :, None] * page_len + jnp.arange(page_len, dtype=jnp.int32)[None, None, :]
    )
    key_count = page_cache.shape[1] * page_len
    usable_pages = (page_used[:, :, None] & (token_place < lengths[:, None, None])).reshape(
        seq_count, key_count
    )
    gathered_keys = page_cache[..., :head_dim].reshape(seq_count, key_count, head_dim)
    gathered_values = page_cache[..., head_dim:].reshape(seq_count, key_count, head_dim)
    scores = (
        jnp.einsum("shd,skd->shk", group_query, gathered_keys, preferred_element_type=jnp.float32)
        * scaling
    )
    scores = jnp.where(usable_pages[:, None, :], scores, NEG_FILL)
    newest_entry = lax.dynamic_index_in_dim(newest_key_value, kv_index, 1, keepdims=False)
    fresh_score = (
        jnp.einsum(
            "shd,sd->sh",
            group_query,
            newest_entry[:, :head_dim],
            preferred_element_type=jnp.float32,
        )
        * scaling
    )
    leading = quarter == 0
    fresh_score = jnp.where(leading, fresh_score, NEG_FILL)
    running_max = jnp.maximum(jnp.max(scores, axis=2), fresh_score)
    weights = jnp.where(usable_pages[:, None, :], jnp.exp(scores - running_max[..., None]), 0.0)
    fresh_weight = jnp.where(leading, jnp.exp(fresh_score - running_max), 0.0)
    running_sum = jnp.sum(weights, axis=2) + fresh_weight
    weighted = jnp.einsum(
        "shk,skd->shd",
        weights.astype(jnp.bfloat16),
        gathered_values,
        preferred_element_type=jnp.float32,
    )
    weighted = weighted + fresh_weight.astype(jnp.bfloat16).astype(jnp.float32)[
        ..., None
    ] * newest_entry[:, None, head_dim:].astype(jnp.float32)
    packed = jnp.concatenate([weighted, running_max[..., None], running_sum[..., None]], axis=2)
    bit_count = group_size.bit_length() - 1
    for bit_index in reversed(range(bit_count)):
        half_heads = packed.shape[1] // 2
        keep_half = quarter >> bit_index & 1
        kept = lax.dynamic_slice_in_dim(packed, keep_half * half_heads, half_heads, 1)
        sent = lax.dynamic_slice_in_dim(packed, (1 - keep_half) * half_heads, half_heads, 1)
        partner = from_partner(sent, "head", bit_index)
        packed = merge_packed(kept, partner, head_dim)
    attention = (
        (packed[..., :head_dim] / packed[..., head_dim + 1 :])
        .reshape(seq_count, block_cols)
        .astype(jnp.bfloat16)
    )
    cols_dev = residual.shape[1]
    all_attention = gathered_copies(attention, "batch", 0)
    head_terms = jnp.dot(all_attention, out_weight, preferred_element_type=jnp.float32)
    projected = taken_together(head_terms.astype(jnp.bfloat16), ("sect", "head")).astype(
        jnp.float32
    )
    hidden_state = residual.astype(jnp.float32) + projected
    token_count, top_count = expert_ids.shape
    capacity = 2 * token_count * top_count // EXPERTS
    pair_local = gate_up_weight.shape[0]
    flat_ids = expert_ids.reshape(-1)
    one_hot = (flat_ids[:, None] == jnp.arange(EXPERTS, dtype=jnp.int32)[None, :]).astype(jnp.int32)
    earlier = jnp.cumsum(one_hot, axis=0) - one_hot
    rank_in = jnp.sum(earlier * one_hot, axis=1)
    sub_half = lax.axis_index("head") // (head_size // 2)
    pair_first = lax.axis_index("sect") * (batch_size * pair_local)
    local_pair = flat_ids // 2 - pair_first
    in_sect = (local_pair >= 0) & (local_pair < batch_size * pair_local)
    full_slot = (
        (local_pair // pair_local * 2 + flat_ids % 2) * pair_local + local_pair % pair_local
    ) * capacity + rank_in
    full_slot = jnp.where(in_sect, full_slot, -1)
    slot_dev = pair_local * capacity
    slot_total = batch_size * 2 * slot_dev
    send_count = batch_size * slot_dev
    matches = (
        full_slot.reshape(token_count, top_count)[None, :, :]
        == jnp.arange(slot_total, dtype=jnp.int32)[:, None, None]
    )
    selector_full = (
        jnp.any(matches, axis=2).astype(jnp.bfloat16).reshape(batch_size, 2, slot_dev, token_count)
    )
    selector = lax.dynamic_index_in_dim(selector_full, sub_half, 1, keepdims=False).reshape(
        send_count, token_count
    )
    coefficient = route_weight / jnp.sum(route_weight, axis=1, keepdims=True)
    combine_full = jnp.sum(jnp.where(matches, coefficient[None, :, :], 0.0), axis=2).T
    scaled = (hidden_state * norm_gain[None, :]).astype(jnp.bfloat16)
    square_parts = split_three(jnp.sum(hidden_state * hidden_state, axis=1))
    outgoing = jnp.dot(selector, scaled, preferred_element_type=jnp.float32).astype(jnp.bfloat16)
    slot_squares = jnp.dot(square_parts, selector.T, preferred_element_type=jnp.float32)
    square_block = jnp.pad(
        jnp.moveaxis(slot_squares.astype(jnp.bfloat16).reshape(3, batch_size, slot_dev), 0, 1),
        ((0, 0), (0, 0), (0, cols_dev - slot_dev)),
    )
    outgoing = jnp.concatenate(
        [outgoing.reshape(batch_size, slot_dev, cols_dev), square_block], axis=1
    )
    arrived = lax.all_to_all(outgoing, "batch", split_axis=0, concat_axis=0, tiled=True)
    rows = arrived[:, :slot_dev].reshape(batch_size, pair_local, capacity, cols_dev)
    got_squares = arrived[:, slot_dev:, :slot_dev].astype(jnp.float32)
    squares = jnp.sum(got_squares, axis=(0, 1))
    inverse = lax.rsqrt(squares / D + NORM_EPS).reshape(pair_local, capacity)
    mixture = jnp.einsum(
        "becd,ebdgf->ecgf",
        rows,
        gate_up_weight.reshape(pair_local, batch_size, cols_dev, *gate_up_weight.shape[2:]),
        preferred_element_type=jnp.float32,
    )
    mixture = mixture * inverse[:, :, None, None]
    activated = (jax.nn.silu(mixture[:, :, 0]) * mixture[:, :, 1]).astype(jnp.bfloat16)
    expert_part = jnp.einsum(
        "ecf,efd->ecd", activated, down_weight, preferred_element_type=jnp.float32
    )
    leaving = expert_part.reshape(1, slot_dev, batch_size, cols_dev)
    came_back = (
        lax.all_to_all(
            leaving.astype(jnp.bfloat16), "batch", split_axis=2, concat_axis=0, tiled=True
        )
        .astype(leaving.dtype)
        .reshape(send_count, cols_dev)
    )
    weights_used = lax.dynamic_index_in_dim(
        combine_full.reshape(token_count, batch_size, 2, slot_dev), sub_half, 2, keepdims=False
    )
    weights_used = weights_used.reshape(token_count, send_count)
    combined = jnp.dot(weights_used, came_back, preferred_element_type=jnp.float32)
    expert_mix = taken_together(combined.astype(jnp.bfloat16), ("sect", "head")).astype(jnp.float32)
    return (hidden_state + expert_mix).astype(jnp.bfloat16)


def solution(mesh):
    placed = (
        P("batch", "head", "sect"),
        P("batch", None, None),
        P("batch", ("sect", "head"), None, None),
        P("batch"),
        P("batch", None, None),
        P(("sect", "head"), "batch"),
        P(None, "batch"),
        P("batch"),
        P(),
        P(),
        P(("sect", "batch"), None, None, "head"),
        P(("sect", "batch"), "head", None),
    )
    return jax.shard_map(
        on_device, mesh=mesh, in_specs=placed, out_specs=P(None, "batch"), check_vma=False
    )
```

```python
import math

import jax
import jax.numpy as jnp
from jax import lax
from jax.sharding import PartitionSpec as P

D = 4096
EXPERTS = 64


NEG_FILL = -1e30
NORM_EPS = 1e-06


def copy_for_each(shard, axis):
    copies = jnp.broadcast_to(shard, (lax.axis_size(axis), *shard.shape))
    return lax.all_to_all(copies, axis, split_axis=0, concat_axis=0, tiled=True)


def in_order(pieces, dim):
    lengths = list(pieces.shape[1:])
    lengths[dim] *= pieces.shape[0]
    return jnp.moveaxis(pieces, 0, dim).reshape(lengths)


def gathered_copies(shard, axis, dim):
    pieces = copy_for_each(shard, axis)
    return in_order(pieces, dim)


def from_partner(shard, axis, distance):
    return lax.ppermute(shard, axis, [(i, i ^ 1 << distance) for i in range(lax.axis_size(axis))])


def taken_together(shard, axis):
    return copy_for_each(shard, axis).astype(jnp.float32).sum(axis=0)


def of_everyone(shard, axis):
    return copy_for_each(shard, axis).sum(axis=0)


def merge_pair(first, second):
    first_max, first_sum, first_acc = first
    second_max, second_sum, second_acc = second
    joined = jnp.maximum(first_max, second_max)
    first_factor = jnp.exp(first_max - joined)
    second_factor = jnp.exp(second_max - joined)
    return (
        joined,
        first_sum * first_factor + second_sum * second_factor,
        first_acc * first_factor[..., None] + second_acc * second_factor[..., None],
    )


def split_three(value):
    high = lax.reduce_precision(value, exponent_bits=8, mantissa_bits=7)
    rest = value - high
    middle = lax.reduce_precision(rest, exponent_bits=8, mantissa_bits=7)
    low = rest - middle
    return jnp.stack([high, middle, low]).astype(jnp.bfloat16)


def merge_packed(first, second, width):
    first_max, first_sum = first[..., width], first[..., width + 1]
    second_max, second_sum = second[..., width], second[..., width + 1]
    joined = jnp.maximum(first_max, second_max)
    first_factor = jnp.exp(first_max - joined)
    second_factor = jnp.exp(second_max - joined)
    return jnp.concatenate(
        [
            first[..., :width] * first_factor[..., None] + second[..., :width] * second_factor[..., None],
            joined[..., None],
            (first_sum * first_factor + second_sum * second_factor)[..., None],
        ],
        axis=-1,
    )


def head_slice(partial_value, begin_at, span_size):
    return tuple(
        (lax.dynamic_slice_in_dim(member, begin_at, span_size, 1) for member in partial_value)
    )


def on_device(
    queries,
    newest_key_value,
    page_cache,
    lengths,
    page_ids,
    out_weight,
    residual,
    norm_gain,
    expert_ids,
    route_weight,
    gate_up_weight,
    down_weight,
):
    seq_count = queries.shape[0]
    head_dim = newest_key_value.shape[2] // 2
    kv_heads = newest_key_value.shape[1]
    sect_size = lax.axis_size("sect")
    head_size = lax.axis_size("head")
    batch_size = lax.axis_size("batch")
    group_size = sect_size * head_size // kv_heads
    position = lax.axis_index("sect") * head_size + lax.axis_index("head")
    kv_index = position // group_size
    quarter = position % group_size
    local_pages = page_cache.shape[1]
    page_len = page_cache.shape[2]
    scaling = 1.0 / math.sqrt(head_dim)
    kv_per_sect = kv_heads // sect_size
    by_kv = jnp.moveaxis(queries.reshape(*queries.shape[:2], kv_per_sect, head_dim), 2, 0)
    per_target = jnp.broadcast_to(
        by_kv[:, None], (kv_per_sect, head_size // kv_per_sect, *by_kv.shape[1:])
    ).reshape(head_size, *by_kv.shape[1:])
    group_query = in_order(
        lax.all_to_all(per_target, "head", split_axis=0, concat_axis=0, tiled=True), 1
    )
    heads_dev = group_query.shape[1] // group_size
    block_cols = heads_dev * head_dim
    chosen = lax.dynamic_index_in_dim(page_ids, kv_index, 1, keepdims=False)
    leading_page = quarter * local_pages
    page_number = jnp.broadcast_to(
        leading_page + jnp.arange(local_pages, dtype=jnp.int32), (seq_count, local_pages)
    )
    page_used = jnp.any(chosen[:, :, None] == page_number[:, None, :], axis=1)
    token_place = (
        page_number[:, :, None] * page_len + jnp.arange(page_len, dtype=jnp.int32)[None, None, :]
    )
    key_count = page_cache.shape[1] * page_len
    usable_pages = (page_used[:, :, None] & (token_place < lengths[:, None, None])).reshape(
        seq_count, key_count
    )
    gathered_keys = page_cache[..., :head_dim].reshape(seq_count, key_count, head_dim)
    gathered_values = page_cache[..., head_dim:].reshape(seq_count, key_count, head_dim)
    scores = (
        jnp.einsum("shd,skd->shk", group_query, gathered_keys, preferred_element_type=jnp.float32)
        * scaling
    )
    scores = jnp.where(usable_pages[:, None, :], scores, NEG_FILL)
    newest_entry = lax.dynamic_index_in_dim(newest_key_value, kv_index, 1, keepdims=False)
    fresh_score = (
        jnp.einsum(
            "shd,sd->sh",
            group_query,
            newest_entry[:, :head_dim],
            preferred_element_type=jnp.float32,
        )
        * scaling
    )
    leading = quarter == 0
    fresh_score = jnp.where(leading, fresh_score, NEG_FILL)
    running_max = jnp.maximum(jnp.max(scores, axis=2), fresh_score)
    weights = jnp.where(usable_pages[:, None, :], jnp.exp(scores - running_max[..., None]), 0.0)
    fresh_weight = jnp.where(leading, jnp.exp(fresh_score - running_max), 0.0)
    running_sum = jnp.sum(weights, axis=2) + fresh_weight
    weighted = jnp.einsum(
        "shk,skd->shd",
        weights.astype(jnp.bfloat16),
        gathered_values,
        preferred_element_type=jnp.float32,
    )
    weighted = weighted + fresh_weight.astype(jnp.bfloat16).astype(jnp.float32)[
        ..., None
    ] * newest_entry[:, None, head_dim:].astype(jnp.float32)
    packed = jnp.concatenate([weighted, running_max[..., None], running_sum[..., None]], axis=2)
    bit_count = group_size.bit_length() - 1
    packed = packed.reshape(seq_count, *([2] * bit_count), heads_dev, head_dim + 2)
    for bit_index in range(bit_count):
        bit_axis = bit_count - bit_index
        keep_half = quarter >> bit_index & 1
        kept = lax.dynamic_index_in_dim(packed, keep_half, bit_axis, keepdims=False)
        sent = lax.dynamic_index_in_dim(packed, 1 - keep_half, bit_axis, keepdims=False)
        partner = from_partner(sent, "head", bit_index)
        packed = merge_packed(kept, partner, head_dim)
    attention = (
        (packed[..., :head_dim] / packed[..., head_dim + 1 :])
        .reshape(seq_count, block_cols)
        .astype(jnp.bfloat16)
    )
    cols_dev = residual.shape[1]
    all_attention = gathered_copies(attention, "batch", 0)
    head_terms = jnp.dot(all_attention, out_weight, preferred_element_type=jnp.float32)
    projected = taken_together(head_terms.astype(jnp.bfloat16), ("sect", "head")).astype(
        jnp.float32
    )
    hidden_state = residual.astype(jnp.float32) + projected
    token_count, top_count = expert_ids.shape
    capacity = 2 * token_count * top_count // EXPERTS
    pair_local = gate_up_weight.shape[0]
    flat_ids = expert_ids.reshape(-1)
    one_hot = (flat_ids[:, None] == jnp.arange(EXPERTS, dtype=jnp.int32)[None, :]).astype(jnp.int32)
    earlier = jnp.cumsum(one_hot, axis=0) - one_hot
    rank_in = jnp.sum(earlier * one_hot, axis=1)
    sub_half = lax.axis_index("head") // (head_size // 2)
    pair_first = lax.axis_index("sect") * (batch_size * pair_local)
    local_pair = flat_ids // 2 - pair_first
    in_sect = (local_pair >= 0) & (local_pair < batch_size * pair_local)
    full_slot = (
        (local_pair // pair_local * 2 + flat_ids % 2) * pair_local + local_pair % pair_local
    ) * capacity + rank_in
    full_slot = jnp.where(in_sect, full_slot, -1)
    slot_dev = pair_local * capacity
    slot_total = batch_size * 2 * slot_dev
    send_count = batch_size * slot_dev
    matches = (
        full_slot.reshape(token_count, top_count)[None, :, :]
        == jnp.arange(slot_total, dtype=jnp.int32)[:, None, None]
    )
    selector_full = (
        jnp.any(matches, axis=2).astype(jnp.bfloat16).reshape(batch_size, 2, slot_dev, token_count)
    )
    selector = lax.dynamic_index_in_dim(selector_full, sub_half, 1, keepdims=False).reshape(
        send_count, token_count
    )
    coefficient = route_weight / jnp.sum(route_weight, axis=1, keepdims=True)
    combine_full = jnp.sum(jnp.where(matches, coefficient[None, :, :], 0.0), axis=2).T
    scaled = (hidden_state * norm_gain[None, :]).astype(jnp.bfloat16)
    square_parts = split_three(jnp.sum(hidden_state * hidden_state, axis=1))
    outgoing = jnp.dot(selector, scaled, preferred_element_type=jnp.float32).astype(jnp.bfloat16)
    slot_squares = jnp.dot(square_parts, selector.T, preferred_element_type=jnp.float32)
    square_block = jnp.pad(
        jnp.moveaxis(slot_squares.astype(jnp.bfloat16).reshape(3, batch_size, slot_dev), 0, 1),
        ((0, 0), (0, 0), (0, cols_dev - slot_dev)),
    )
    outgoing = jnp.concatenate(
        [outgoing.reshape(batch_size, slot_dev, cols_dev), square_block], axis=1
    )
    arrived = lax.all_to_all(outgoing, "batch", split_axis=0, concat_axis=0, tiled=True)
    rows = arrived[:, :slot_dev].reshape(batch_size, pair_local, capacity, cols_dev)
    got_squares = arrived[:, slot_dev:, :slot_dev].astype(jnp.float32)
    squares = jnp.sum(got_squares, axis=(0, 1))
    inverse = lax.rsqrt(squares / D + NORM_EPS).reshape(pair_local, capacity)
    mixture = jnp.einsum(
        "becd,ebdgf->ecgf",
        rows,
        gate_up_weight.reshape(pair_local, batch_size, cols_dev, *gate_up_weight.shape[2:]),
        preferred_element_type=jnp.float32,
    )
    mixture = mixture * inverse[:, :, None, None]
    activated = (jax.nn.silu(mixture[:, :, 0]) * mixture[:, :, 1]).astype(jnp.bfloat16)
    expert_part = jnp.einsum(
        "ecf,efd->ecd", activated, down_weight, preferred_element_type=jnp.float32
    )
    leaving = expert_part.reshape(1, slot_dev, batch_size, cols_dev)
    came_back = (
        lax.all_to_all(
            leaving.astype(jnp.bfloat16), "batch", split_axis=2, concat_axis=0, tiled=True
        )
        .astype(leaving.dtype)
        .reshape(send_count, cols_dev)
    )
    weights_used = lax.dynamic_index_in_dim(
        combine_full.reshape(token_count, batch_size, 2, slot_dev), sub_half, 2, keepdims=False
    )
    weights_used = weights_used.reshape(token_count, send_count)
    combined = jnp.dot(weights_used, came_back, preferred_element_type=jnp.float32)
    expert_mix = taken_together(combined.astype(jnp.bfloat16), ("sect", "head")).astype(jnp.float32)
    return (hidden_state + expert_mix).astype(jnp.bfloat16)


def solution(mesh):
    placed = (
        P("batch", "head", "sect"),
        P("batch", None, None),
        P("batch", ("sect", "head"), None, None),
        P("batch"),
        P("batch", None, None),
        P(("sect", "head"), "batch"),
        P(None, "batch"),
        P("batch"),
        P(),
        P(),
        P(("sect", "batch"), None, None, "head"),
        P(("sect", "batch"), "head", None),
    )
    return jax.shard_map(
        on_device, mesh=mesh, in_specs=placed, out_specs=P(None, "batch"), check_vma=False
    )
```

```python
import math

import jax
import jax.numpy as jnp
from jax import lax
from jax.sharding import PartitionSpec as P

D = 4096
EXPERTS = 64


NEG_FILL = -1e30
NORM_EPS = 1e-06


def copy_for_each(shard, axis):
    copies = jnp.broadcast_to(shard, (lax.axis_size(axis), *shard.shape))
    return lax.all_to_all(copies, axis, split_axis=0, concat_axis=0, tiled=True)


def in_order(pieces, dim):
    lengths = list(pieces.shape[1:])
    lengths[dim] *= pieces.shape[0]
    return jnp.moveaxis(pieces, 0, dim).reshape(lengths)


def gathered_copies(shard, axis, dim):
    pieces = copy_for_each(shard, axis)
    return in_order(pieces, dim)


def from_partner(shard, axis, distance):
    return lax.ppermute(shard, axis, [(i, i ^ 1 << distance) for i in range(lax.axis_size(axis))])


def taken_together(shard, axis):
    return copy_for_each(shard, axis).astype(jnp.float32).sum(axis=0)


def doubled_sum(shard, axis):
    count = lax.axis_size(axis)
    step = 1
    while step < count:
        partner = lax.ppermute(shard, axis, [(i, i ^ step) for i in range(count)])
        shard = lax.reduce_precision(shard + partner, exponent_bits=8, mantissa_bits=7)
        step *= 2
    return shard


def of_everyone(shard, axis):
    return copy_for_each(shard, axis).sum(axis=0)


def merge_pair(first, second):
    first_max, first_sum, first_acc = first
    second_max, second_sum, second_acc = second
    joined = jnp.maximum(first_max, second_max)
    first_factor = jnp.exp(first_max - joined)
    second_factor = jnp.exp(second_max - joined)
    return (
        joined,
        first_sum * first_factor + second_sum * second_factor,
        first_acc * first_factor[..., None] + second_acc * second_factor[..., None],
    )


def split_three(value):
    high = lax.reduce_precision(value, exponent_bits=8, mantissa_bits=7)
    rest = value - high
    middle = lax.reduce_precision(rest, exponent_bits=8, mantissa_bits=7)
    low = rest - middle
    return jnp.stack([high, middle, low]).astype(jnp.bfloat16)


def merge_packed(first, second, width):
    first_max, first_sum = first[..., width], first[..., width + 1]
    second_max, second_sum = second[..., width], second[..., width + 1]
    joined = jnp.maximum(first_max, second_max)
    first_factor = jnp.exp(first_max - joined)
    second_factor = jnp.exp(second_max - joined)
    return jnp.concatenate(
        [
            first[..., :width] * first_factor[..., None] + second[..., :width] * second_factor[..., None],
            joined[..., None],
            (first_sum * first_factor + second_sum * second_factor)[..., None],
        ],
        axis=2,
    )


def head_slice(partial_value, begin_at, span_size):
    return tuple(
        (lax.dynamic_slice_in_dim(member, begin_at, span_size, 1) for member in partial_value)
    )


def on_device(
    queries,
    newest_key_value,
    page_cache,
    lengths,
    page_ids,
    out_weight,
    residual,
    norm_gain,
    expert_ids,
    route_weight,
    gate_up_weight,
    down_weight,
):
    seq_count = queries.shape[0]
    head_dim = newest_key_value.shape[2] // 2
    kv_heads = newest_key_value.shape[1]
    sect_size = lax.axis_size("sect")
    head_size = lax.axis_size("head")
    batch_size = lax.axis_size("batch")
    group_size = sect_size * head_size // kv_heads
    position = lax.axis_index("sect") * head_size + lax.axis_index("head")
    kv_index = position // group_size
    quarter = position % group_size
    local_pages = page_cache.shape[1]
    page_len = page_cache.shape[2]
    scaling = 1.0 / math.sqrt(head_dim)
    kv_per_sect = kv_heads // sect_size
    by_kv = jnp.moveaxis(queries.reshape(*queries.shape[:2], kv_per_sect, head_dim), 2, 0)
    per_target = jnp.broadcast_to(
        by_kv[:, None], (kv_per_sect, head_size // kv_per_sect, *by_kv.shape[1:])
    ).reshape(head_size, *by_kv.shape[1:])
    group_query = in_order(
        lax.all_to_all(per_target, "head", split_axis=0, concat_axis=0, tiled=True), 1
    )
    heads_dev = group_query.shape[1] // group_size
    block_cols = heads_dev * head_dim
    chosen = lax.dynamic_index_in_dim(page_ids, kv_index, 1, keepdims=False)
    leading_page = quarter * local_pages
    page_number = jnp.broadcast_to(
        leading_page + jnp.arange(local_pages, dtype=jnp.int32), (seq_count, local_pages)
    )
    page_used = jnp.any(chosen[:, :, None] == page_number[:, None, :], axis=1)
    token_place = (
        page_number[:, :, None] * page_len + jnp.arange(page_len, dtype=jnp.int32)[None, None, :]
    )
    key_count = page_cache.shape[1] * page_len
    usable_pages = (page_used[:, :, None] & (token_place < lengths[:, None, None])).reshape(
        seq_count, key_count
    )
    gathered_keys = page_cache[..., :head_dim].reshape(seq_count, key_count, head_dim)
    gathered_values = page_cache[..., head_dim:].reshape(seq_count, key_count, head_dim)
    scores = (
        jnp.einsum("shd,skd->shk", group_query, gathered_keys, preferred_element_type=jnp.float32)
        * scaling
    )
    scores = jnp.where(usable_pages[:, None, :], scores, NEG_FILL)
    newest_entry = lax.dynamic_index_in_dim(newest_key_value, kv_index, 1, keepdims=False)
    fresh_score = (
        jnp.einsum(
            "shd,sd->sh",
            group_query,
            newest_entry[:, :head_dim],
            preferred_element_type=jnp.float32,
        )
        * scaling
    )
    leading = quarter == 0
    fresh_score = jnp.where(leading, fresh_score, NEG_FILL)
    running_max = jnp.maximum(jnp.max(scores, axis=2), fresh_score)
    weights = jnp.where(usable_pages[:, None, :], jnp.exp(scores - running_max[..., None]), 0.0)
    fresh_weight = jnp.where(leading, jnp.exp(fresh_score - running_max), 0.0)
    running_sum = jnp.sum(weights, axis=2) + fresh_weight
    weighted = jnp.einsum(
        "shk,skd->shd",
        weights.astype(jnp.bfloat16),
        gathered_values,
        preferred_element_type=jnp.float32,
    )
    weighted = weighted + fresh_weight.astype(jnp.bfloat16).astype(jnp.float32)[
        ..., None
    ] * newest_entry[:, None, head_dim:].astype(jnp.float32)
    packed = jnp.concatenate([weighted, running_max[..., None], running_sum[..., None]], axis=2)
    bit_count = group_size.bit_length() - 1
    for bit_index in reversed(range(bit_count)):
        half_heads = packed.shape[1] // 2
        keep_half = quarter >> bit_index & 1
        kept = lax.dynamic_slice_in_dim(packed, keep_half * half_heads, half_heads, 1)
        sent = lax.dynamic_slice_in_dim(packed, (1 - keep_half) * half_heads, half_heads, 1)
        partner = from_partner(sent, "head", bit_index)
        packed = merge_packed(kept, partner, head_dim)
    attention = (
        (packed[..., :head_dim] / packed[..., head_dim + 1 :])
        .reshape(seq_count, block_cols)
        .astype(jnp.bfloat16)
    )
    cols_dev = residual.shape[1]
    all_attention = gathered_copies(attention, "batch", 0)
    head_terms = jnp.dot(all_attention, out_weight, preferred_element_type=jnp.float32)
    projected = doubled_sum(head_terms.astype(jnp.bfloat16), ("sect", "head")).astype(
        jnp.float32
    )
    hidden_state = residual.astype(jnp.float32) + projected
    token_count, top_count = expert_ids.shape
    capacity = 2 * token_count * top_count // EXPERTS
    pair_local = gate_up_weight.shape[0]
    flat_ids = expert_ids.reshape(-1)
    one_hot = (flat_ids[:, None] == jnp.arange(EXPERTS, dtype=jnp.int32)[None, :]).astype(jnp.int32)
    earlier = jnp.cumsum(one_hot, axis=0) - one_hot
    rank_in = jnp.sum(earlier * one_hot, axis=1)
    sub_half = lax.axis_index("head") // (head_size // 2)
    pair_first = lax.axis_index("sect") * (batch_size * pair_local)
    local_pair = flat_ids // 2 - pair_first
    in_sect = (local_pair >= 0) & (local_pair < batch_size * pair_local)
    full_slot = (
        (local_pair // pair_local * 2 + flat_ids % 2) * pair_local + local_pair % pair_local
    ) * capacity + rank_in
    full_slot = jnp.where(in_sect, full_slot, -1)
    slot_dev = pair_local * capacity
    slot_total = batch_size * 2 * slot_dev
    send_count = batch_size * slot_dev
    matches = (
        full_slot.reshape(token_count, top_count)[None, :, :]
        == jnp.arange(slot_total, dtype=jnp.int32)[:, None, None]
    )
    selector_full = (
        jnp.any(matches, axis=2).astype(jnp.bfloat16).reshape(batch_size, 2, slot_dev, token_count)
    )
    selector = lax.dynamic_index_in_dim(selector_full, sub_half, 1, keepdims=False).reshape(
        send_count, token_count
    )
    coefficient = route_weight / jnp.sum(route_weight, axis=1, keepdims=True)
    combine_full = jnp.sum(jnp.where(matches, coefficient[None, :, :], 0.0), axis=2).T
    scaled = (hidden_state * norm_gain[None, :]).astype(jnp.bfloat16)
    square_parts = split_three(jnp.sum(hidden_state * hidden_state, axis=1))
    outgoing = jnp.dot(selector, scaled, preferred_element_type=jnp.float32).astype(jnp.bfloat16)
    slot_squares = jnp.dot(square_parts, selector.T, preferred_element_type=jnp.float32)
    square_block = jnp.pad(
        jnp.moveaxis(slot_squares.astype(jnp.bfloat16).reshape(3, batch_size, slot_dev), 0, 1),
        ((0, 0), (0, 0), (0, cols_dev - slot_dev)),
    )
    outgoing = jnp.concatenate(
        [outgoing.reshape(batch_size, slot_dev, cols_dev), square_block], axis=1
    )
    arrived = lax.all_to_all(outgoing, "batch", split_axis=0, concat_axis=0, tiled=True)
    rows = arrived[:, :slot_dev].reshape(batch_size, pair_local, capacity, cols_dev)
    got_squares = arrived[:, slot_dev:, :slot_dev].astype(jnp.float32)
    squares = jnp.sum(got_squares, axis=(0, 1))
    inverse = lax.rsqrt(squares / D + NORM_EPS).reshape(pair_local, capacity)
    mixture = jnp.einsum(
        "becd,ebdgf->ecgf",
        rows,
        gate_up_weight.reshape(pair_local, batch_size, cols_dev, *gate_up_weight.shape[2:]),
        preferred_element_type=jnp.float32,
    )
    mixture = mixture * inverse[:, :, None, None]
    activated = (jax.nn.silu(mixture[:, :, 0]) * mixture[:, :, 1]).astype(jnp.bfloat16)
    expert_part = jnp.einsum(
        "ecf,efd->ecd", activated, down_weight, preferred_element_type=jnp.float32
    )
    leaving = expert_part.reshape(1, slot_dev, batch_size, cols_dev)
    came_back = (
        lax.all_to_all(
            leaving.astype(jnp.bfloat16), "batch", split_axis=2, concat_axis=0, tiled=True
        )
        .astype(leaving.dtype)
        .reshape(send_count, cols_dev)
    )
    weights_used = lax.dynamic_index_in_dim(
        combine_full.reshape(token_count, batch_size, 2, slot_dev), sub_half, 2, keepdims=False
    )
    weights_used = weights_used.reshape(token_count, send_count)
    combined = jnp.dot(weights_used, came_back, preferred_element_type=jnp.float32)
    expert_mix = doubled_sum(combined.astype(jnp.bfloat16), ("sect", "head")).astype(jnp.float32)
    return (hidden_state + expert_mix).astype(jnp.bfloat16)


def solution(mesh):
    placed = (
        P("batch", "head", "sect"),
        P("batch", None, None),
        P("batch", ("sect", "head"), None, None),
        P("batch"),
        P("batch", None, None),
        P(("sect", "head"), "batch"),
        P(None, "batch"),
        P("batch"),
        P(),
        P(),
        P(("sect", "batch"), None, None, "head"),
        P(("sect", "batch"), "head", None),
    )
    return jax.shard_map(
        on_device, mesh=mesh, in_specs=placed, out_specs=P(None, "batch"), check_vma=False
    )
```

```python
import math

import jax
import jax.numpy as jnp
from jax import lax
from jax.sharding import PartitionSpec as P

D = 4096
EXPERTS = 64


NEG_FILL = -1e30
NORM_EPS = 1e-06


def copy_for_each(shard, axis):
    copies = jnp.broadcast_to(shard, (lax.axis_size(axis), *shard.shape))
    return lax.all_to_all(copies, axis, split_axis=0, concat_axis=0, tiled=True)


def in_order(pieces, dim):
    lengths = list(pieces.shape[1:])
    lengths[dim] *= pieces.shape[0]
    return jnp.moveaxis(pieces, 0, dim).reshape(lengths)


def gathered_copies(shard, axis, dim):
    pieces = copy_for_each(shard, axis)
    return in_order(pieces, dim)


def from_partner(shard, axis, distance):
    return lax.ppermute(shard, axis, [(i, i ^ 1 << distance) for i in range(lax.axis_size(axis))])


def taken_together(shard, axis):
    return copy_for_each(shard, axis).astype(jnp.float32).sum(axis=0)


def doubled_sum(shard, axis, steps):
    count = lax.axis_size(axis)
    for step in steps:
        partner = lax.ppermute(shard, axis, [(i, i ^ step) for i in range(count)])
        shard = lax.reduce_precision(shard + partner, exponent_bits=8, mantissa_bits=7)
    return shard


def neighbour_steps(head_size):
    return (head_size, head_size + 1, 2, 6)


def of_everyone(shard, axis):
    return copy_for_each(shard, axis).sum(axis=0)


def merge_pair(first, second):
    first_max, first_sum, first_acc = first
    second_max, second_sum, second_acc = second
    joined = jnp.maximum(first_max, second_max)
    first_factor = jnp.exp(first_max - joined)
    second_factor = jnp.exp(second_max - joined)
    return (
        joined,
        first_sum * first_factor + second_sum * second_factor,
        first_acc * first_factor[..., None] + second_acc * second_factor[..., None],
    )


def split_three(value):
    high = lax.reduce_precision(value, exponent_bits=8, mantissa_bits=7)
    rest = value - high
    middle = lax.reduce_precision(rest, exponent_bits=8, mantissa_bits=7)
    low = rest - middle
    return jnp.stack([high, middle, low]).astype(jnp.bfloat16)


def merge_packed(first, second, width):
    first_max, first_sum = first[..., width], first[..., width + 1]
    second_max, second_sum = second[..., width], second[..., width + 1]
    joined = jnp.maximum(first_max, second_max)
    first_factor = jnp.exp(first_max - joined)
    second_factor = jnp.exp(second_max - joined)
    return jnp.concatenate(
        [
            first[..., :width] * first_factor[..., None] + second[..., :width] * second_factor[..., None],
            joined[..., None],
            (first_sum * first_factor + second_sum * second_factor)[..., None],
        ],
        axis=2,
    )


def head_slice(partial_value, begin_at, span_size):
    return tuple(
        (lax.dynamic_slice_in_dim(member, begin_at, span_size, 1) for member in partial_value)
    )


def on_device(
    queries,
    newest_key_value,
    page_cache,
    lengths,
    page_ids,
    out_weight,
    residual,
    norm_gain,
    expert_ids,
    route_weight,
    gate_up_weight,
    down_weight,
):
    seq_count = queries.shape[0]
    head_dim = newest_key_value.shape[2] // 2
    kv_heads = newest_key_value.shape[1]
    sect_size = lax.axis_size("sect")
    head_size = lax.axis_size("head")
    batch_size = lax.axis_size("batch")
    group_size = sect_size * head_size // kv_heads
    position = lax.axis_index("sect") * head_size + lax.axis_index("head")
    kv_index = position // group_size
    quarter = position % group_size
    local_pages = page_cache.shape[1]
    page_len = page_cache.shape[2]
    scaling = 1.0 / math.sqrt(head_dim)
    kv_per_sect = kv_heads // sect_size
    by_kv = jnp.moveaxis(queries.reshape(*queries.shape[:2], kv_per_sect, head_dim), 2, 0)
    per_target = jnp.broadcast_to(
        by_kv[:, None], (kv_per_sect, head_size // kv_per_sect, *by_kv.shape[1:])
    ).reshape(head_size, *by_kv.shape[1:])
    group_query = in_order(
        lax.all_to_all(per_target, "head", split_axis=0, concat_axis=0, tiled=True), 1
    )
    heads_dev = group_query.shape[1] // group_size
    block_cols = heads_dev * head_dim
    chosen = lax.dynamic_index_in_dim(page_ids, kv_index, 1, keepdims=False)
    leading_page = quarter * local_pages
    page_number = jnp.broadcast_to(
        leading_page + jnp.arange(local_pages, dtype=jnp.int32), (seq_count, local_pages)
    )
    page_used = jnp.any(chosen[:, :, None] == page_number[:, None, :], axis=1)
    token_place = (
        page_number[:, :, None] * page_len + jnp.arange(page_len, dtype=jnp.int32)[None, None, :]
    )
    key_count = page_cache.shape[1] * page_len
    usable_pages = (page_used[:, :, None] & (token_place < lengths[:, None, None])).reshape(
        seq_count, key_count
    )
    gathered_keys = page_cache[..., :head_dim].reshape(seq_count, key_count, head_dim)
    gathered_values = page_cache[..., head_dim:].reshape(seq_count, key_count, head_dim)
    scores = (
        jnp.einsum("shd,skd->shk", group_query, gathered_keys, preferred_element_type=jnp.float32)
        * scaling
    )
    scores = jnp.where(usable_pages[:, None, :], scores, NEG_FILL)
    newest_entry = lax.dynamic_index_in_dim(newest_key_value, kv_index, 1, keepdims=False)
    fresh_score = (
        jnp.einsum(
            "shd,sd->sh",
            group_query,
            newest_entry[:, :head_dim],
            preferred_element_type=jnp.float32,
        )
        * scaling
    )
    leading = quarter == 0
    fresh_score = jnp.where(leading, fresh_score, NEG_FILL)
    running_max = jnp.maximum(jnp.max(scores, axis=2), fresh_score)
    weights = jnp.where(usable_pages[:, None, :], jnp.exp(scores - running_max[..., None]), 0.0)
    fresh_weight = jnp.where(leading, jnp.exp(fresh_score - running_max), 0.0)
    running_sum = jnp.sum(weights, axis=2) + fresh_weight
    weighted = jnp.einsum(
        "shk,skd->shd",
        weights.astype(jnp.bfloat16),
        gathered_values,
        preferred_element_type=jnp.float32,
    )
    weighted = weighted + fresh_weight.astype(jnp.bfloat16).astype(jnp.float32)[
        ..., None
    ] * newest_entry[:, None, head_dim:].astype(jnp.float32)
    packed = jnp.concatenate([weighted, running_max[..., None], running_sum[..., None]], axis=2)
    bit_count = group_size.bit_length() - 1
    for bit_index in reversed(range(bit_count)):
        half_heads = packed.shape[1] // 2
        keep_half = quarter >> bit_index & 1
        kept = lax.dynamic_slice_in_dim(packed, keep_half * half_heads, half_heads, 1)
        sent = lax.dynamic_slice_in_dim(packed, (1 - keep_half) * half_heads, half_heads, 1)
        partner = from_partner(sent, "head", bit_index)
        packed = merge_packed(kept, partner, head_dim)
    attention = (
        (packed[..., :head_dim] / packed[..., head_dim + 1 :])
        .reshape(seq_count, block_cols)
        .astype(jnp.bfloat16)
    )
    cols_dev = residual.shape[1]
    all_attention = gathered_copies(attention, "batch", 0)
    head_terms = jnp.dot(all_attention, out_weight, preferred_element_type=jnp.float32)
    projected = doubled_sum(
        head_terms.astype(jnp.bfloat16), ("sect", "head"), neighbour_steps(head_size)
    ).astype(
        jnp.float32
    )
    hidden_state = residual.astype(jnp.float32) + projected
    token_count, top_count = expert_ids.shape
    capacity = 2 * token_count * top_count // EXPERTS
    pair_local = gate_up_weight.shape[0]
    flat_ids = expert_ids.reshape(-1)
    one_hot = (flat_ids[:, None] == jnp.arange(EXPERTS, dtype=jnp.int32)[None, :]).astype(jnp.int32)
    earlier = jnp.cumsum(one_hot, axis=0) - one_hot
    rank_in = jnp.sum(earlier * one_hot, axis=1)
    sub_half = lax.axis_index("head") // (head_size // 2)
    pair_first = lax.axis_index("sect") * (batch_size * pair_local)
    local_pair = flat_ids // 2 - pair_first
    in_sect = (local_pair >= 0) & (local_pair < batch_size * pair_local)
    full_slot = (
        (local_pair // pair_local * 2 + flat_ids % 2) * pair_local + local_pair % pair_local
    ) * capacity + rank_in
    full_slot = jnp.where(in_sect, full_slot, -1)
    slot_dev = pair_local * capacity
    slot_total = batch_size * 2 * slot_dev
    send_count = batch_size * slot_dev
    matches = (
        full_slot.reshape(token_count, top_count)[None, :, :]
        == jnp.arange(slot_total, dtype=jnp.int32)[:, None, None]
    )
    selector_full = (
        jnp.any(matches, axis=2).astype(jnp.bfloat16).reshape(batch_size, 2, slot_dev, token_count)
    )
    selector = lax.dynamic_index_in_dim(selector_full, sub_half, 1, keepdims=False).reshape(
        send_count, token_count
    )
    coefficient = route_weight / jnp.sum(route_weight, axis=1, keepdims=True)
    combine_full = jnp.sum(jnp.where(matches, coefficient[None, :, :], 0.0), axis=2).T
    scaled = (hidden_state * norm_gain[None, :]).astype(jnp.bfloat16)
    square_parts = split_three(jnp.sum(hidden_state * hidden_state, axis=1))
    outgoing = jnp.dot(selector, scaled, preferred_element_type=jnp.float32).astype(jnp.bfloat16)
    slot_squares = jnp.dot(square_parts, selector.T, preferred_element_type=jnp.float32)
    square_block = jnp.pad(
        jnp.moveaxis(slot_squares.astype(jnp.bfloat16).reshape(3, batch_size, slot_dev), 0, 1),
        ((0, 0), (0, 0), (0, cols_dev - slot_dev)),
    )
    outgoing = jnp.concatenate(
        [outgoing.reshape(batch_size, slot_dev, cols_dev), square_block], axis=1
    )
    arrived = lax.all_to_all(outgoing, "batch", split_axis=0, concat_axis=0, tiled=True)
    rows = arrived[:, :slot_dev].reshape(batch_size, pair_local, capacity, cols_dev)
    got_squares = arrived[:, slot_dev:, :slot_dev].astype(jnp.float32)
    squares = jnp.sum(got_squares, axis=(0, 1))
    inverse = lax.rsqrt(squares / D + NORM_EPS).reshape(pair_local, capacity)
    mixture = jnp.einsum(
        "becd,ebdgf->ecgf",
        rows,
        gate_up_weight.reshape(pair_local, batch_size, cols_dev, *gate_up_weight.shape[2:]),
        preferred_element_type=jnp.float32,
    )
    mixture = mixture * inverse[:, :, None, None]
    activated = (jax.nn.silu(mixture[:, :, 0]) * mixture[:, :, 1]).astype(jnp.bfloat16)
    expert_part = jnp.einsum(
        "ecf,efd->ecd", activated, down_weight, preferred_element_type=jnp.float32
    )
    leaving = expert_part.reshape(1, slot_dev, batch_size, cols_dev)
    came_back = (
        lax.all_to_all(
            leaving.astype(jnp.bfloat16), "batch", split_axis=2, concat_axis=0, tiled=True
        )
        .astype(leaving.dtype)
        .reshape(send_count, cols_dev)
    )
    weights_used = lax.dynamic_index_in_dim(
        combine_full.reshape(token_count, batch_size, 2, slot_dev), sub_half, 2, keepdims=False
    )
    weights_used = weights_used.reshape(token_count, send_count)
    combined = jnp.dot(weights_used, came_back, preferred_element_type=jnp.float32)
    expert_mix = doubled_sum(
        combined.astype(jnp.bfloat16), ("sect", "head"), neighbour_steps(head_size)
    ).astype(jnp.float32)
    return (hidden_state + expert_mix).astype(jnp.bfloat16)


def solution(mesh):
    placed = (
        P("batch", "head", "sect"),
        P("batch", None, None),
        P("batch", ("sect", "head"), None, None),
        P("batch"),
        P("batch", None, None),
        P(("sect", "head"), "batch"),
        P(None, "batch"),
        P("batch"),
        P(),
        P(),
        P(("sect", "batch"), None, None, "head"),
        P(("sect", "batch"), "head", None),
    )
    return jax.shard_map(
        on_device, mesh=mesh, in_specs=placed, out_specs=P(None, "batch"), check_vma=False
    )
```

```python
import math

import jax
import jax.numpy as jnp
from jax import lax
from jax.sharding import PartitionSpec as P

D = 4096
EXPERTS = 64


NEG_FILL = -1e30
NORM_EPS = 1e-06


def copy_for_each(shard, axis):
    copies = jnp.broadcast_to(shard, (lax.axis_size(axis), *shard.shape))
    return lax.all_to_all(copies, axis, split_axis=0, concat_axis=0, tiled=True)


def in_order(pieces, dim):
    lengths = list(pieces.shape[1:])
    lengths[dim] *= pieces.shape[0]
    return jnp.moveaxis(pieces, 0, dim).reshape(lengths)


def gathered_copies(shard, axis, dim):
    pieces = copy_for_each(shard, axis)
    return in_order(pieces, dim)


def from_partner(shard, axis, distance):
    return lax.ppermute(shard, axis, [(i, i ^ 1 << distance) for i in range(lax.axis_size(axis))])


def taken_together(shard, axis):
    return copy_for_each(shard, axis).astype(jnp.float32).sum(axis=0)


def doubled_sum(shard, axis, steps):
    count = lax.axis_size(axis)
    for step in steps:
        partner = lax.ppermute(shard, axis, [(i, i ^ step) for i in range(count)])
        shard = lax.reduce_precision(shard + partner, exponent_bits=8, mantissa_bits=7)
    return shard


def neighbour_steps(head_size):
    return (head_size, head_size + 1, 2, 6)


def of_everyone(shard, axis):
    return copy_for_each(shard, axis).sum(axis=0)


def merge_pair(first, second):
    first_max, first_sum, first_acc = first
    second_max, second_sum, second_acc = second
    joined = jnp.maximum(first_max, second_max)
    first_factor = jnp.exp(first_max - joined)
    second_factor = jnp.exp(second_max - joined)
    return (
        joined,
        first_sum * first_factor + second_sum * second_factor,
        first_acc * first_factor[..., None] + second_acc * second_factor[..., None],
    )


def split_three(value):
    high = lax.reduce_precision(value, exponent_bits=8, mantissa_bits=7)
    rest = value - high
    middle = lax.reduce_precision(rest, exponent_bits=8, mantissa_bits=7)
    low = rest - middle
    return jnp.stack([high, middle, low]).astype(jnp.bfloat16)


def merge_packed(first, second, width):
    first_max, first_sum = first[..., width], first[..., width + 1]
    second_max, second_sum = second[..., width], second[..., width + 1]
    joined = jnp.maximum(first_max, second_max)
    first_factor = jnp.exp(first_max - joined)
    second_factor = jnp.exp(second_max - joined)
    return jnp.concatenate(
        [
            first[..., :width] * first_factor[..., None] + second[..., :width] * second_factor[..., None],
            joined[..., None],
            (first_sum * first_factor + second_sum * second_factor)[..., None],
        ],
        axis=2,
    )


def head_slice(partial_value, begin_at, span_size):
    return tuple(
        (lax.dynamic_slice_in_dim(member, begin_at, span_size, 1) for member in partial_value)
    )


def on_device(
    queries,
    newest_key_value,
    page_cache,
    lengths,
    page_ids,
    out_weight,
    residual,
    norm_gain,
    expert_ids,
    route_weight,
    gate_up_weight,
    down_weight,
):
    seq_count = queries.shape[0]
    head_dim = newest_key_value.shape[2] // 2
    kv_heads = newest_key_value.shape[1]
    sect_size = lax.axis_size("sect")
    head_size = lax.axis_size("head")
    batch_size = lax.axis_size("batch")
    group_size = sect_size * head_size // kv_heads
    position = lax.axis_index("sect") * head_size + lax.axis_index("head")
    kv_index = position // group_size
    quarter = position % group_size
    local_pages = page_cache.shape[1]
    page_len = page_cache.shape[2]
    scaling = 1.0 / math.sqrt(head_dim)
    kv_per_sect = kv_heads // sect_size
    own_slot = (jnp.arange(head_size) == lax.axis_index("head")).astype(queries.dtype)
    collected = own_slot[:, None, None, None] * queries[None]
    for step in (2, 6, 1):
        collected = collected + lax.ppermute(
            collected, "head", [(i, i ^ step) for i in range(head_size)]
        )
    kv_local = kv_index % kv_per_sect
    group_query = in_order(
        lax.dynamic_slice_in_dim(collected, kv_local * head_dim, head_dim, 3), 1
    )
    heads_dev = group_query.shape[1] // group_size
    block_cols = heads_dev * head_dim
    chosen = lax.dynamic_index_in_dim(page_ids, kv_index, 1, keepdims=False)
    leading_page = quarter * local_pages
    page_number = jnp.broadcast_to(
        leading_page + jnp.arange(local_pages, dtype=jnp.int32), (seq_count, local_pages)
    )
    page_used = jnp.any(chosen[:, :, None] == page_number[:, None, :], axis=1)
    token_place = (
        page_number[:, :, None] * page_len + jnp.arange(page_len, dtype=jnp.int32)[None, None, :]
    )
    key_count = page_cache.shape[1] * page_len
    usable_pages = (page_used[:, :, None] & (token_place < lengths[:, None, None])).reshape(
        seq_count, key_count
    )
    gathered_keys = page_cache[..., :head_dim].reshape(seq_count, key_count, head_dim)
    gathered_values = page_cache[..., head_dim:].reshape(seq_count, key_count, head_dim)
    scores = (
        jnp.einsum("shd,skd->shk", group_query, gathered_keys, preferred_element_type=jnp.float32)
        * scaling
    )
    scores = jnp.where(usable_pages[:, None, :], scores, NEG_FILL)
    newest_entry = lax.dynamic_index_in_dim(newest_key_value, kv_index, 1, keepdims=False)
    fresh_score = (
        jnp.einsum(
            "shd,sd->sh",
            group_query,
            newest_entry[:, :head_dim],
            preferred_element_type=jnp.float32,
        )
        * scaling
    )
    leading = quarter == 0
    fresh_score = jnp.where(leading, fresh_score, NEG_FILL)
    running_max = jnp.maximum(jnp.max(scores, axis=2), fresh_score)
    weights = jnp.where(usable_pages[:, None, :], jnp.exp(scores - running_max[..., None]), 0.0)
    fresh_weight = jnp.where(leading, jnp.exp(fresh_score - running_max), 0.0)
    running_sum = jnp.sum(weights, axis=2) + fresh_weight
    weighted = jnp.einsum(
        "shk,skd->shd",
        weights.astype(jnp.bfloat16),
        gathered_values,
        preferred_element_type=jnp.float32,
    )
    weighted = weighted + fresh_weight.astype(jnp.bfloat16).astype(jnp.float32)[
        ..., None
    ] * newest_entry[:, None, head_dim:].astype(jnp.float32)
    packed = jnp.concatenate([weighted, running_max[..., None], running_sum[..., None]], axis=2)
    bit_count = group_size.bit_length() - 1
    for bit_index in reversed(range(bit_count)):
        half_heads = packed.shape[1] // 2
        keep_half = quarter >> bit_index & 1
        kept = lax.dynamic_slice_in_dim(packed, keep_half * half_heads, half_heads, 1)
        sent = lax.dynamic_slice_in_dim(packed, (1 - keep_half) * half_heads, half_heads, 1)
        partner = from_partner(sent, "head", bit_index)
        packed = merge_packed(kept, partner, head_dim)
    attention = (
        (packed[..., :head_dim] / packed[..., head_dim + 1 :])
        .reshape(seq_count, block_cols)
        .astype(jnp.bfloat16)
    )
    cols_dev = residual.shape[1]
    all_attention = gathered_copies(attention, "batch", 0)
    head_terms = jnp.dot(all_attention, out_weight, preferred_element_type=jnp.float32)
    projected = doubled_sum(
        head_terms.astype(jnp.bfloat16), ("sect", "head"), neighbour_steps(head_size)
    ).astype(
        jnp.float32
    )
    hidden_state = residual.astype(jnp.float32) + projected
    token_count, top_count = expert_ids.shape
    capacity = 2 * token_count * top_count // EXPERTS
    pair_local = gate_up_weight.shape[0]
    flat_ids = expert_ids.reshape(-1)
    one_hot = (flat_ids[:, None] == jnp.arange(EXPERTS, dtype=jnp.int32)[None, :]).astype(jnp.int32)
    earlier = jnp.cumsum(one_hot, axis=0) - one_hot
    rank_in = jnp.sum(earlier * one_hot, axis=1)
    sub_half = lax.axis_index("head") // (head_size // 2)
    pair_first = lax.axis_index("sect") * (batch_size * pair_local)
    local_pair = flat_ids // 2 - pair_first
    in_sect = (local_pair >= 0) & (local_pair < batch_size * pair_local)
    full_slot = (
        (local_pair // pair_local * 2 + flat_ids % 2) * pair_local + local_pair % pair_local
    ) * capacity + rank_in
    full_slot = jnp.where(in_sect, full_slot, -1)
    slot_dev = pair_local * capacity
    slot_total = batch_size * 2 * slot_dev
    send_count = batch_size * slot_dev
    matches = (
        full_slot.reshape(token_count, top_count)[None, :, :]
        == jnp.arange(slot_total, dtype=jnp.int32)[:, None, None]
    )
    selector_full = (
        jnp.any(matches, axis=2).astype(jnp.bfloat16).reshape(batch_size, 2, slot_dev, token_count)
    )
    selector = lax.dynamic_index_in_dim(selector_full, sub_half, 1, keepdims=False).reshape(
        send_count, token_count
    )
    coefficient = route_weight / jnp.sum(route_weight, axis=1, keepdims=True)
    combine_full = jnp.sum(jnp.where(matches, coefficient[None, :, :], 0.0), axis=2).T
    scaled = (hidden_state * norm_gain[None, :]).astype(jnp.bfloat16)
    square_parts = split_three(jnp.sum(hidden_state * hidden_state, axis=1))
    outgoing = jnp.dot(selector, scaled, preferred_element_type=jnp.float32).astype(jnp.bfloat16)
    slot_squares = jnp.dot(square_parts, selector.T, preferred_element_type=jnp.float32)
    square_block = jnp.pad(
        jnp.moveaxis(slot_squares.astype(jnp.bfloat16).reshape(3, batch_size, slot_dev), 0, 1),
        ((0, 0), (0, 0), (0, cols_dev - slot_dev)),
    )
    outgoing = jnp.concatenate(
        [outgoing.reshape(batch_size, slot_dev, cols_dev), square_block], axis=1
    )
    arrived = lax.all_to_all(outgoing, "batch", split_axis=0, concat_axis=0, tiled=True)
    rows = arrived[:, :slot_dev].reshape(batch_size, pair_local, capacity, cols_dev)
    got_squares = arrived[:, slot_dev:, :slot_dev].astype(jnp.float32)
    squares = jnp.sum(got_squares, axis=(0, 1))
    inverse = lax.rsqrt(squares / D + NORM_EPS).reshape(pair_local, capacity)
    mixture = jnp.einsum(
        "becd,ebdgf->ecgf",
        rows,
        gate_up_weight.reshape(pair_local, batch_size, cols_dev, *gate_up_weight.shape[2:]),
        preferred_element_type=jnp.float32,
    )
    mixture = mixture * inverse[:, :, None, None]
    activated = (jax.nn.silu(mixture[:, :, 0]) * mixture[:, :, 1]).astype(jnp.bfloat16)
    expert_part = jnp.einsum(
        "ecf,efd->ecd", activated, down_weight, preferred_element_type=jnp.float32
    )
    leaving = expert_part.reshape(1, slot_dev, batch_size, cols_dev)
    came_back = (
        lax.all_to_all(
            leaving.astype(jnp.bfloat16), "batch", split_axis=2, concat_axis=0, tiled=True
        )
        .astype(leaving.dtype)
        .reshape(send_count, cols_dev)
    )
    weights_used = lax.dynamic_index_in_dim(
        combine_full.reshape(token_count, batch_size, 2, slot_dev), sub_half, 2, keepdims=False
    )
    weights_used = weights_used.reshape(token_count, send_count)
    combined = jnp.dot(weights_used, came_back, preferred_element_type=jnp.float32)
    expert_mix = doubled_sum(
        combined.astype(jnp.bfloat16), ("sect", "head"), neighbour_steps(head_size)
    ).astype(jnp.float32)
    return (hidden_state + expert_mix).astype(jnp.bfloat16)


def solution(mesh):
    placed = (
        P("batch", "head", "sect"),
        P("batch", None, None),
        P("batch", ("sect", "head"), None, None),
        P("batch"),
        P("batch", None, None),
        P(("sect", "head"), "batch"),
        P(None, "batch"),
        P("batch"),
        P(),
        P(),
        P(("sect", "batch"), None, None, "head"),
        P(("sect", "batch"), "head", None),
    )
    return jax.shard_map(
        on_device, mesh=mesh, in_specs=placed, out_specs=P(None, "batch"), check_vma=False
    )
```
